32 devices in a mesh: group: 4 (over z), member: 8 (over y, x, core).
Axes of the slice: x: 2, y: 2, z: 4, core: 2. Of those that a mesh axis runs over, the one named last changes fastest.
Arguments:
- query_feat: bfloat16 [4096, 4096], P(('group', 'member'))
- code_feat: bfloat16 [4096, 4096], P(('group', 'member'))
- projection: bfloat16 [4096, 1024], replicated
- hard_ids: int32 [32, 16], P(('group', 'member')), may hold values from 0 to 63, as said below
- loss_weight: float32 [4096], P(('group', 'member')), may hold values from 1 to 4
Outputs:
- query_grad: bfloat16 [4096, 4096], P(('group', 'member'))
- code_grad: bfloat16 [4096, 4096], P(('group', 'member'))
- projection_grad: float32 [4096, 1024], P(('group', 'member'))
The draws below stay inside these ranges and needn't reach their ends.
Inputs may be any that keep to these rules, and one draw needn't show every extreme that they name: `hard_ids`: entry (owner device g * 8 + m) * 2 + slot names code rows of that device. A row names 16 different blocks, none of its own group; at most 8 of them lie in one group, and exactly 8 in some group of every row.
All inputs are finite; a program needn't handle non-finite values.
Results may differ from the reference program's by a relative error of at most 0.02.
Values may be sent and summed in bfloat16 or wider, within the bound.
No kernel may reach another device: no remote copies, remote signals or barrier semaphores. Data moves between devices by JAX's collectives and lax.ppermute only.
A program may use at most 128 MiB of HBM per device.

```python
import math
import jax
import jax.numpy as jnp
from jax import lax

D = 4096
E = 1024
QB = 128
CB = 64
HARD = 16
CAP = 8
PAIRS = 4096
N_GROUP = 4
N_MEMBER = 8


def row_scales(key):
    return jnp.exp(jax.random.uniform(key, (PAIRS, 1), jnp.float32, math.log(0.2), math.log(2.0)))


def code_features(key):
    array_shape = (PAIRS, D)
    scales = row_scales(jax.random.fold_in(key, 102))
    values = jax.random.normal(jax.random.fold_in(key, 101), array_shape, jnp.float32)
    return values * scales


def draw_code_feat(key, part):
    return code_features(key).astype(jnp.bfloat16)


def draw_query_feat(key, part):
    array_shape = (PAIRS, D)
    scales = row_scales(jax.random.fold_in(key, 202))
    values = jax.random.normal(jax.random.fold_in(key, 201), array_shape, jnp.float32) * scales
    return values.astype(jnp.bfloat16)


def draw_projection(key, part):
    values = jax.random.normal(jax.random.fold_in(key, 302), (D, E), jnp.float32)
    column_scale = jnp.exp(jax.random.uniform(jax.random.fold_in(key, 301), (1, E), jnp.float32, math.log(4.0), math.log(40.0)))
    return (values * column_scale * D ** (-0.5)).astype(jnp.bfloat16)


def draw_hard_ids(key, part):
    devices = N_GROUP * N_MEMBER
    per_group = N_MEMBER * (QB // CB)
    others = N_GROUP - 1
    spill_count = HARD - CAP

    def one_row(row_key, device):
        row_keys = jax.random.split(row_key, 4)
        chosen = jax.random.permutation(row_keys[0], (others - 1) * CAP)[:spill_count].astype(jnp.int32)
        rank_of = jnp.concatenate([jnp.zeros((CAP,), jnp.int32), 1 + chosen // CAP])
        places = jnp.concatenate([jnp.arange(CAP, dtype=jnp.int32), chosen % CAP])
        shuffle_groups = jax.random.permutation(row_keys[1], others).astype(jnp.int32)
        target = (device // N_MEMBER + 1 + shuffle_groups[rank_of]) % N_GROUP
        within = jax.vmap(lambda subkey: jax.random.permutation(subkey, per_group))(jax.random.split(row_keys[2], others)).astype(jnp.int32)
        local_block = within[rank_of, places]
        entries = (target * per_group + local_block).astype(jnp.int32)
        return entries[jax.random.permutation(row_keys[3], HARD)]
    return jax.vmap(one_row)(jax.random.split(key, devices), jnp.arange(devices, dtype=jnp.int32))


def shard_levels(own_key, shape, shards, smallest, largest):
    loudness, own = 1.0, jax.random.fold_in(own_key, 6)
    for dim, parts in shards:
        draws = jnp.exp(jax.random.uniform(jax.random.fold_in(own, dim), (parts,), jnp.float32, smallest / len(shards), largest / len(shards)))
        loudness = loudness * jnp.repeat(draws, shape[dim] // parts).reshape([-1 if axis == dim else 1 for axis in range(len(shape))])
    return loudness


def setup_inputs(seed: int = 0) -> dict:
    seeds = jax.random.split(jax.random.key(seed), 6)
    query_feat = draw_query_feat(jax.random.fold_in(seeds[5], 71), 0)
    code_feat = draw_code_feat(jax.random.fold_in(seeds[5], 71), 0)
    projection = draw_projection(jax.random.fold_in(seeds[5], 71), 0)
    hard_ids = draw_hard_ids(jax.random.fold_in(seeds[5], 71), 0)
    loss_weight = jnp.clip(jnp.exp(math.log(4.0) - 1.3862944 * jax.random.uniform(seeds[4], (PAIRS,), jnp.float32) ** shard_levels(seeds[4], (PAIRS,), ((0, 32),), -0.2, 0.2)), 1.0, 4.0)
    return dict(query_feat=query_feat, code_feat=code_feat, projection=projection, hard_ids=hard_ids, loss_weight=loss_weight)


inverse_temp = 120.0
epsilon = 1e-06

def embed(features, projection):
    values = jnp.dot(features, projection, preferred_element_type=jnp.float32)
    inverse = lax.rsqrt(lax.optimization_barrier(jnp.sum(values * values, axis=1)) + epsilon)
    unit_vec = values * inverse[:, None]
    return (unit_vec, inverse, unit_vec.astype(jnp.bfloat16))

def norm_back(upstream, unit_vec, inverse):
    inner_prod = lax.optimization_barrier(jnp.sum(unit_vec * upstream, axis=1, keepdims=True))
    return (inverse[:, None] * (upstream - unit_vec * inner_prod)).astype(jnp.bfloat16)

def reference(query_feat, code_feat, projection, hard_ids, loss_weight):
    devices = N_GROUP * N_MEMBER
    slot_count = QB // CB
    group_span = N_MEMBER * QB
    q_unit, q_inv, q_emb = embed(query_feat, projection)
    c_unit, c_inv, c_emb = embed(code_feat, projection)
    code_blocks = c_emb.reshape(devices * slot_count, CB, E)
    offsets = jnp.arange(QB, dtype=jnp.int32)
    columns = jnp.arange(group_span, dtype=jnp.int32)

    def one_block(carry, device):
        group_index = device // N_MEMBER
        member_index = device % N_MEMBER
        queries = lax.dynamic_slice_in_dim(q_emb, device * QB, QB, 0)
        weights = lax.dynamic_slice_in_dim(loss_weight, device * QB, QB, 0)
        first_row = group_index * group_span
        in_group = lax.dynamic_slice_in_dim(c_emb, first_row, group_span, 0)
        wanted = lax.dynamic_index_in_dim(hard_ids, device, 0, keepdims=False)
        negatives = code_blocks[wanted].reshape(HARD * CB, E)
        group_scores = inverse_temp * jnp.dot(queries, in_group.T, preferred_element_type=jnp.float32)
        hard_scores = inverse_temp * jnp.dot(queries, negatives.T, preferred_element_type=jnp.float32)
        row_max = jnp.maximum(lax.optimization_barrier(jnp.max(group_scores, axis=1)), lax.optimization_barrier(jnp.max(hard_scores, axis=1)))
        row_sum = lax.optimization_barrier(jnp.sum(jnp.exp(group_scores - row_max[:, None]), axis=1)) + lax.optimization_barrier(jnp.sum(jnp.exp(hard_scores - row_max[:, None]), axis=1))
        log_total = row_max + jnp.log(row_sum)
        factor = weights * inverse_temp
        positive = (columns[None, :] == (member_index * QB + offsets)[:, None]).astype(jnp.float32)
        grad_group = (factor[:, None] * (jnp.exp(group_scores - log_total[:, None]) - positive)).astype(jnp.bfloat16)
        grad_hard = (factor[:, None] * jnp.exp(hard_scores - log_total[:, None])).astype(jnp.bfloat16)
        query_delta = jnp.dot(grad_group, in_group, preferred_element_type=jnp.float32) + jnp.dot(grad_hard, negatives, preferred_element_type=jnp.float32)
        group_terms = jnp.dot(grad_group.T, queries, preferred_element_type=jnp.float32)
        hard_terms = lax.optimization_barrier(jnp.dot(grad_hard.T, queries, preferred_element_type=jnp.float32).astype(jnp.bfloat16)).astype(jnp.float32)
        current = lax.dynamic_slice_in_dim(carry, first_row, group_span, 0)
        carry = lax.dynamic_update_slice_in_dim(carry, current + group_terms, first_row, 0)
        blocked = carry.reshape(devices * slot_count, CB, E).at[wanted].add(hard_terms.reshape(HARD, CB, E))
        return (blocked.reshape(devices * QB, E), query_delta)
    code_delta, query_delta = lax.scan(one_block, jnp.zeros((devices * QB, E), jnp.float32), jnp.arange(devices, dtype=jnp.int32))
    query_delta = query_delta.reshape(devices * QB, E)
    dz_query = norm_back(query_delta, q_unit, q_inv)
    dz_code = norm_back(code_delta, c_unit, c_inv)
    query_grad = jnp.dot(dz_query, projection.T, preferred_element_type=jnp.float32).astype(jnp.bfloat16)
    code_grad = jnp.dot(dz_code, projection.T, preferred_element_type=jnp.float32).astype(jnp.bfloat16)
    projection_grad = jnp.dot(query_feat.T, dz_query, preferred_element_type=jnp.float32) + jnp.dot(code_feat.T, dz_code, preferred_element_type=jnp.float32)
    return (query_grad, code_grad, projection_grad)
```

```python
import jax
import jax.numpy as jnp
from jax import lax
from jax.sharding import PartitionSpec as P

CB = 64


inverse_temp = 120.0
epsilon = 1e-06


def embed(features, projection):
    values = jnp.dot(features, projection, preferred_element_type=jnp.float32)
    inverse = lax.rsqrt(jnp.sum(values * values, axis=1) + epsilon)
    unit_vec = values * inverse[:, None]
    return (unit_vec, inverse, unit_vec.astype(jnp.bfloat16))


def norm_back(upstream, unit_vec, inverse):
    inner_prod = jnp.sum(unit_vec * upstream, axis=1, keepdims=True)
    return (inverse[:, None] * (upstream - unit_vec * inner_prod)).astype(jnp.bfloat16)


def body(query_feat, code_feat, projection, hard_ids, loss_weight):
    groups = lax.axis_size("group")
    members = lax.axis_size("member")
    group_index = lax.axis_index("group")
    member_index = lax.axis_index("member")
    queries_dev = query_feat.shape[0]
    feat_width = query_feat.shape[1]
    emb_width = projection.shape[1]
    slot_count = queries_dev // CB
    per_group = members * slot_count
    group_span = members * queries_dev
    rows_dev = feat_width // (groups * members)

    feats = jnp.stack([query_feat, code_feat], axis=0).reshape(
        2, queries_dev, groups, members, rows_dev
    )
    feats = jnp.transpose(feats, (3, 0, 1, 2, 4))
    feat_cols = lax.all_to_all(feats, "member", split_axis=0, concat_axis=0, tiled=True)

    q_unit, q_inv, q_emb = embed(query_feat, projection)
    c_unit, c_inv, c_emb = embed(code_feat, projection)
    group_codes = lax.all_gather(c_emb, "member", axis=0, tiled=True)
    q_all = lax.all_gather(q_emb, "group", axis=0)
    ids_all = lax.all_gather(hard_ids[0], "group", axis=0)
    w_all = lax.all_gather(loss_weight, "group", axis=0)

    block_ids = group_index * per_group + jnp.arange(per_group, dtype=jnp.int32)
    asked = jnp.any(ids_all[:, :, None] == block_ids[None, None, :], axis=1)
    own = jnp.arange(groups, dtype=jnp.int32) == group_index
    block_mask = asked | own[:, None]
    col_mask = jnp.broadcast_to(
        block_mask[:, :, None], (groups, per_group, CB)
    ).reshape(groups, 1, group_span)

    scores = inverse_temp * jnp.einsum(
        "gqe,ke->gqk", q_all, group_codes, preferred_element_type=jnp.float32
    )
    scores = jnp.where(col_mask, scores, -jnp.inf)
    part_max = jnp.max(scores, axis=2)
    safe_max = jnp.where(part_max > -jnp.inf, part_max, 0.0)
    part_sum = jnp.sum(jnp.exp(scores - safe_max[:, :, None]), axis=2)
    stats = lax.all_gather(jnp.stack([part_max, part_sum], axis=0), "group", axis=0)
    row_max = jnp.max(stats[:, 0], axis=0)
    row_sum = jnp.sum(stats[:, 1] * jnp.exp(stats[:, 0] - row_max[None]), axis=0)
    log_total = row_max + jnp.log(row_sum)

    offsets = jnp.arange(queries_dev, dtype=jnp.int32)
    columns = jnp.arange(group_span, dtype=jnp.int32)
    positive = (columns[None, :] == (member_index * queries_dev + offsets)[:, None]).astype(
        jnp.float32
    )
    positive = positive[None] * own[:, None, None].astype(jnp.float32)
    factor = w_all * inverse_temp
    grad = (
        factor[:, :, None] * (jnp.exp(scores - log_total[:, :, None]) - positive)
    ).astype(jnp.bfloat16)

    delta_parts = jnp.einsum("gqk,ke->gqe", grad, group_codes, preferred_element_type=jnp.float32)
    query_delta = lax.psum_scatter(delta_parts, "group", scatter_dimension=0, tiled=True).reshape(
        queries_dev, emb_width
    )

    code_terms = None
    for g in range(groups):
        term = jnp.dot(grad[g].T, q_all[g], preferred_element_type=jnp.float32)
        term = jnp.where(g == group_index, term, term.astype(jnp.bfloat16).astype(jnp.float32))
        code_terms = term if code_terms is None else code_terms + term
    code_delta = lax.psum_scatter(
        code_terms.astype(jnp.bfloat16), "member", scatter_dimension=0, tiled=True
    ).astype(jnp.float32)

    dz_query = norm_back(query_delta, q_unit, q_inv)
    dz_code = norm_back(code_delta, c_unit, c_inv)
    query_grad = jnp.einsum(
        "qe,de->qd", dz_query, projection, preferred_element_type=jnp.float32
    ).astype(jnp.bfloat16)
    code_grad = jnp.einsum(
        "qe,de->qd", dz_code, projection, preferred_element_type=jnp.float32
    ).astype(jnp.bfloat16)

    dz_all = lax.all_gather(jnp.stack([dz_query, dz_code], axis=0), "member", axis=0)
    proj_parts = jnp.einsum(
        "mtqgr,mtqe->gre", feat_cols, dz_all, preferred_element_type=jnp.float32
    )
    projection_grad = lax.psum_scatter(
        proj_parts, "group", scatter_dimension=0, tiled=True
    ).reshape(rows_dev, emb_width)
    return (query_grad, code_grad, projection_grad)


def solution(mesh):
    return jax.shard_map(
        body,
        mesh=mesh,
        in_specs=(
            P(("group", "member"), None),
            P(("group", "member"), None),
            P(),
            P(("group", "member"), None),
            P(("group", "member")),
        ),
        out_specs=(
            P(("group", "member"), None),
            P(("group", "member"), None),
            P(("group", "member"), None),
        ),
        check_vma=False,
    )
```

```python
import jax
import jax.numpy as jnp
from jax import lax
from jax.sharding import PartitionSpec as P

CB = 64


inverse_temp = 120.0
epsilon = 1e-06


def embed(features, projection):
    values = jnp.dot(features, projection, preferred_element_type=jnp.float32)
    inverse = lax.rsqrt(jnp.sum(values * values, axis=1) + epsilon)
    unit_vec = values * inverse[:, None]
    return (unit_vec, inverse, unit_vec.astype(jnp.bfloat16))


def norm_back(upstream, unit_vec, inverse):
    inner_prod = jnp.sum(unit_vec * upstream, axis=1, keepdims=True)
    return (inverse[:, None] * (upstream - unit_vec * inner_prod)).astype(jnp.bfloat16)


def shift_all(x, axis):
    size = lax.axis_size(axis)
    index = lax.axis_index(axis)
    got = [x]
    for s in range(1, size):
        got.append(lax.ppermute(x, axis, [(i, (i + s) % size) for i in range(size)]))
    order = (index - jnp.arange(size)) % size
    return jax.tree.map(lambda *xs: jnp.take(jnp.stack(xs, axis=0), order, axis=0), *got)


def exchange(parts, axis):
    size = lax.axis_size(axis)
    index = lax.axis_index(axis)
    got = [jnp.take(parts, index, axis=0)]
    for s in range(1, size):
        sent = jnp.take(parts, (index + s) % size, axis=0)
        got.append(lax.ppermute(sent, axis, [(i, (i + s) % size) for i in range(size)]))
    stacked = jnp.stack(got, axis=0)
    return jnp.take(stacked, (index - jnp.arange(size)) % size, axis=0)


def body(query_feat, code_feat, projection, hard_ids, loss_weight):
    groups = lax.axis_size("group")
    members = lax.axis_size("member")
    group_index = lax.axis_index("group")
    member_index = lax.axis_index("member")
    queries_dev = query_feat.shape[0]
    feat_width = query_feat.shape[1]
    emb_width = projection.shape[1]
    slot_count = queries_dev // CB
    per_group = members * slot_count
    group_span = members * queries_dev
    rows_dev = feat_width // (groups * members)

    feats = jnp.stack([query_feat, code_feat], axis=0).reshape(
        2, queries_dev, groups, members, rows_dev
    )
    feats = jnp.transpose(feats, (3, 0, 1, 2, 4))
    feat_cols = exchange(feats, "member")

    q_unit, q_inv, q_emb = embed(query_feat, projection)
    c_unit, c_inv, c_emb = embed(code_feat, projection)
    group_codes = lax.all_gather(c_emb, "member", axis=0, tiled=True)
    q_all, ids_all, w_all = shift_all((q_emb, hard_ids[0], loss_weight), "group")

    block_ids = group_index * per_group + jnp.arange(per_group, dtype=jnp.int32)
    asked = jnp.any(ids_all[:, :, None] == block_ids[None, None, :], axis=1)
    own = jnp.arange(groups, dtype=jnp.int32) == group_index
    block_mask = asked | own[:, None]
    col_mask = jnp.broadcast_to(
        block_mask[:, :, None], (groups, per_group, CB)
    ).reshape(groups, 1, group_span)

    scores = inverse_temp * jnp.einsum(
        "gqe,ke->gqk", q_all, group_codes, preferred_element_type=jnp.float32
    )
    scores = jnp.where(col_mask, scores, -jnp.inf)
    part_max = jnp.max(scores, axis=2)
    safe_max = jnp.where(part_max > -jnp.inf, part_max, 0.0)
    part_sum = jnp.sum(jnp.exp(scores - safe_max[:, :, None]), axis=2)
    stats = shift_all(jnp.stack([part_max, part_sum], axis=0), "group")
    row_max = jnp.max(stats[:, 0], axis=0)
    row_sum = jnp.sum(stats[:, 1] * jnp.exp(stats[:, 0] - row_max[None]), axis=0)
    log_total = row_max + jnp.log(row_sum)

    offsets = jnp.arange(queries_dev, dtype=jnp.int32)
    columns = jnp.arange(group_span, dtype=jnp.int32)
    positive = (columns[None, :] == (member_index * queries_dev + offsets)[:, None]).astype(
        jnp.float32
    )
    positive = positive[None] * own[:, None, None].astype(jnp.float32)
    factor = w_all * inverse_temp
    grad = (
        factor[:, :, None] * (jnp.exp(scores - log_total[:, :, None]) - positive)
    ).astype(jnp.bfloat16)

    delta_parts = jnp.einsum("gqk,ke->gqe", grad, group_codes, preferred_element_type=jnp.float32)
    returned = exchange(delta_parts.astype(jnp.bfloat16), "group").astype(jnp.float32)
    own_part = jnp.take(delta_parts, group_index, axis=0)
    query_delta = own_part + jnp.sum(jnp.where(own[:, None, None], 0.0, returned), axis=0)

    code_terms = None
    for g in range(groups):
        term = jnp.dot(grad[g].T, q_all[g], preferred_element_type=jnp.float32)
        term = jnp.where(g == group_index, term, term.astype(jnp.bfloat16).astype(jnp.float32))
        code_terms = term if code_terms is None else code_terms + term
    code_delta = lax.psum_scatter(
        code_terms.astype(jnp.bfloat16), "member", scatter_dimension=0, tiled=True
    ).astype(jnp.float32)

    dz_query = norm_back(query_delta, q_unit, q_inv)
    dz_code = norm_back(code_delta, c_unit, c_inv)
    query_grad = jnp.einsum(
        "qe,de->qd", dz_query, projection, preferred_element_type=jnp.float32
    ).astype(jnp.bfloat16)
    code_grad = jnp.einsum(
        "qe,de->qd", dz_code, projection, preferred_element_type=jnp.float32
    ).astype(jnp.bfloat16)

    dz_all = lax.all_gather(jnp.stack([dz_query, dz_code], axis=0), "member", axis=0)
    proj_parts = jnp.einsum(
        "mtqgr,mtqe->gre", feat_cols, dz_all, preferred_element_type=jnp.float32
    )
    projection_grad = lax.psum_scatter(
        proj_parts, "group", scatter_dimension=0, tiled=True
    ).reshape(rows_dev, emb_width)
    return (query_grad, code_grad, projection_grad)


def solution(mesh):
    return jax.shard_map(
        body,
        mesh=mesh,
        in_specs=(
            P(("group", "member"), None),
            P(("group", "member"), None),
            P(),
            P(("group", "member"), None),
            P(("group", "member")),
        ),
        out_specs=(
            P(("group", "member"), None),
            P(("group", "member"), None),
            P(("group", "member"), None),
        ),
        check_vma=False,
    )
```

```python
import jax
import jax.numpy as jnp
from jax import lax
from jax.sharding import PartitionSpec as P

CB = 64


inverse_temp = 120.0
epsilon = 1e-06


def embed(features, projection):
    values = jnp.dot(features, projection, preferred_element_type=jnp.float32)
    inverse = lax.rsqrt(jnp.sum(values * values, axis=1) + epsilon)
    unit_vec = values * inverse[:, None]
    return (unit_vec, inverse, unit_vec.astype(jnp.bfloat16))


def norm_back(upstream, unit_vec, inverse):
    inner_prod = jnp.sum(unit_vec * upstream, axis=1, keepdims=True)
    return (inverse[:, None] * (upstream - unit_vec * inner_prod)).astype(jnp.bfloat16)


def shift_all(x, axis):
    size = lax.axis_size(axis)
    index = lax.axis_index(axis)
    got = [x]
    for s in range(1, size):
        got.append(lax.ppermute(x, axis, [(i, (i + s) % size) for i in range(size)]))
    order = (index - jnp.arange(size)) % size
    return jax.tree.map(lambda *xs: jnp.take(jnp.stack(xs, axis=0), order, axis=0), *got)


def exchange(parts, axis):
    size = lax.axis_size(axis)
    index = lax.axis_index(axis)
    got = [jnp.take(parts, index, axis=0)]
    for s in range(1, size):
        sent = jnp.take(parts, (index + s) % size, axis=0)
        got.append(lax.ppermute(sent, axis, [(i, (i + s) % size) for i in range(size)]))
    stacked = jnp.stack(got, axis=0)
    return jnp.take(stacked, (index - jnp.arange(size)) % size, axis=0)


def body(query_feat, code_feat, projection, hard_ids, loss_weight):
    groups = lax.axis_size("group")
    members = lax.axis_size("member")
    group_index = lax.axis_index("group")
    member_index = lax.axis_index("member")
    queries_dev = query_feat.shape[0]
    feat_width = query_feat.shape[1]
    emb_width = projection.shape[1]
    slot_count = queries_dev // CB
    per_group = members * slot_count
    group_span = members * queries_dev
    rows_dev = feat_width // (groups * members)

    feats = jnp.stack([query_feat, code_feat], axis=0).reshape(
        2, queries_dev, groups, members, rows_dev
    )
    feats = jnp.transpose(feats, (3, 0, 1, 2, 4))
    feat_cols = exchange(feats, "member")

    q_unit, q_inv, q_emb = embed(query_feat, projection)
    c_unit, c_inv, c_emb = embed(code_feat, projection)
    group_codes = lax.all_gather(c_emb, "member", axis=0, tiled=True)
    q_all, ids_all, w_all = shift_all((q_emb, hard_ids[0], loss_weight), "group")

    block_ids = group_index * per_group + jnp.arange(per_group, dtype=jnp.int32)
    asked = jnp.any(ids_all[:, :, None] == block_ids[None, None, :], axis=1)
    own = jnp.arange(groups, dtype=jnp.int32) == group_index
    block_mask = asked | own[:, None]
    col_mask = jnp.broadcast_to(
        block_mask[:, :, None], (groups, per_group, CB)
    ).reshape(groups, 1, group_span)

    scores = inverse_temp * jnp.einsum(
        "gqe,ke->gqk", q_all, group_codes, preferred_element_type=jnp.float32
    )
    scores = jnp.where(col_mask, scores, -jnp.inf)
    part_max = jnp.max(scores, axis=2)
    safe_max = jnp.where(part_max > -jnp.inf, part_max, 0.0)
    part_sum = jnp.sum(jnp.exp(scores - safe_max[:, :, None]), axis=2)
    stats = shift_all(jnp.stack([part_max, part_sum], axis=0), "group")
    row_max = jnp.max(stats[:, 0], axis=0)
    row_sum = jnp.sum(stats[:, 1] * jnp.exp(stats[:, 0] - row_max[None]), axis=0)
    log_total = row_max + jnp.log(row_sum)

    offsets = jnp.arange(queries_dev, dtype=jnp.int32)
    columns = jnp.arange(group_span, dtype=jnp.int32)
    positive = (columns[None, :] == (member_index * queries_dev + offsets)[:, None]).astype(
        jnp.float32
    )
    positive = positive[None] * own[:, None, None].astype(jnp.float32)
    factor = w_all * inverse_temp
    grad = (
        factor[:, :, None] * (jnp.exp(scores - log_total[:, :, None]) - positive)
    ).astype(jnp.bfloat16)

    delta_parts = jnp.einsum("gqk,ke->gqe", grad, group_codes, preferred_element_type=jnp.float32)
    returned = exchange(delta_parts.astype(jnp.bfloat16), "group").astype(jnp.float32)
    own_part = jnp.take(delta_parts, group_index, axis=0)
    query_delta = own_part + jnp.sum(jnp.where(own[:, None, None], 0.0, returned), axis=0)

    code_terms = None
    for g in range(groups):
        term = jnp.dot(grad[g].T, q_all[g], preferred_element_type=jnp.float32)
        term = jnp.where(g == group_index, term, term.astype(jnp.bfloat16).astype(jnp.float32))
        code_terms = term if code_terms is None else code_terms + term
    code_delta = jnp.sum(
        exchange(code_terms.astype(jnp.bfloat16).reshape(members, queries_dev, emb_width), "member")
        .astype(jnp.float32),
        axis=0,
    )

    dz_query = norm_back(query_delta, q_unit, q_inv)
    dz_code = norm_back(code_delta, c_unit, c_inv)
    query_grad = jnp.einsum(
        "qe,de->qd", dz_query, projection, preferred_element_type=jnp.float32
    ).astype(jnp.bfloat16)
    code_grad = jnp.einsum(
        "qe,de->qd", dz_code, projection, preferred_element_type=jnp.float32
    ).astype(jnp.bfloat16)

    dz_all = shift_all(jnp.stack([dz_query, dz_code], axis=0), "member")
    proj_parts = jnp.einsum(
        "mtqgr,mtqe->gre", feat_cols, dz_all, preferred_element_type=jnp.float32
    )
    proj_back = exchange(proj_parts.astype(jnp.bfloat16), "group").astype(jnp.float32)
    projection_grad = jnp.take(proj_parts, group_index, axis=0) + jnp.sum(
        jnp.where(own[:, None, None], 0.0, proj_back), axis=0
    )
    return (query_grad, code_grad, projection_grad)


def solution(mesh):
    return jax.shard_map(
        body,
        mesh=mesh,
        in_specs=(
            P(("group", "member"), None),
            P(("group", "member"), None),
            P(),
            P(("group", "member"), None),
            P(("group", "member")),
        ),
        out_specs=(
            P(("group", "member"), None),
            P(("group", "member"), None),
            P(("group", "member"), None),
        ),
        check_vma=False,
    )
```

```python
import jax
import jax.numpy as jnp
from jax import lax
from jax.sharding import PartitionSpec as P

CB = 64


inverse_temp = 120.0
epsilon = 1e-06


def embed(features, projection):
    values = jnp.dot(features, projection, preferred_element_type=jnp.float32)
    inverse = lax.rsqrt(jnp.sum(values * values, axis=1) + epsilon)
    unit_vec = values * inverse[:, None]
    return (unit_vec, inverse, unit_vec.astype(jnp.bfloat16))


def norm_back(upstream, unit_vec, inverse):
    inner_prod = jnp.sum(unit_vec * upstream, axis=1, keepdims=True)
    return (inverse[:, None] * (upstream - unit_vec * inner_prod)).astype(jnp.bfloat16)


def shift_all(x, axis):
    size = lax.axis_size(axis)
    index = lax.axis_index(axis)
    got = [x]
    for s in range(1, size):
        got.append(lax.ppermute(x, axis, [(i, (i + s) % size) for i in range(size)]))
    order = (index - jnp.arange(size)) % size
    return jax.tree.map(lambda *xs: jnp.take(jnp.stack(xs, axis=0), order, axis=0), *got)


def exchange(parts, axis):
    size = lax.axis_size(axis)
    index = lax.axis_index(axis)
    got = [jnp.take(parts, index, axis=0)]
    for s in range(1, size):
        sent = jnp.take(parts, (index + s) % size, axis=0)
        got.append(lax.ppermute(sent, axis, [(i, (i + s) % size) for i in range(size)]))
    stacked = jnp.stack(got, axis=0)
    return jnp.take(stacked, (index - jnp.arange(size)) % size, axis=0)


def body(query_feat, code_feat, projection, hard_ids, loss_weight):
    groups = lax.axis_size("group")
    members = lax.axis_size("member")
    group_index = lax.axis_index("group")
    member_index = lax.axis_index("member")
    queries_dev = query_feat.shape[0]
    feat_width = query_feat.shape[1]
    emb_width = projection.shape[1]
    slot_count = queries_dev // CB
    per_group = members * slot_count
    group_span = members * queries_dev
    rows_dev = feat_width // (groups * members)

    feats = jnp.stack([query_feat, code_feat], axis=0).reshape(
        2, queries_dev, groups, members, rows_dev
    )
    feats = jnp.transpose(feats, (3, 0, 1, 2, 4))
    feat_cols = exchange(feats, "member")

    q_unit, q_inv, q_emb = embed(query_feat, projection)
    c_unit, c_inv, c_emb = embed(code_feat, projection)
    group_codes = lax.all_gather(c_emb, "member", axis=0, tiled=True)
    q_all, ids_all, w_all = shift_all((q_emb, hard_ids[0], loss_weight), "group")

    block_ids = group_index * per_group + jnp.arange(per_group, dtype=jnp.int32)
    asked = jnp.any(ids_all[:, :, None] == block_ids[None, None, :], axis=1)
    own = jnp.arange(groups, dtype=jnp.int32) == group_index
    block_mask = asked | own[:, None]
    col_mask = jnp.broadcast_to(
        block_mask[:, :, None], (groups, per_group, CB)
    ).reshape(groups, 1, group_span)

    scores = inverse_temp * jnp.einsum(
        "gqe,ke->gqk", q_all, group_codes, preferred_element_type=jnp.float32
    )
    scores = jnp.where(col_mask, scores, -jnp.inf)
    part_max = jnp.max(scores, axis=2)
    safe_max = jnp.where(part_max > -jnp.inf, part_max, 0.0)
    part_sum = jnp.sum(jnp.exp(scores - safe_max[:, :, None]), axis=2)
    stats = shift_all(jnp.stack([part_max, part_sum], axis=0), "group")
    row_max = jnp.max(stats[:, 0], axis=0)
    row_sum = jnp.sum(stats[:, 1] * jnp.exp(stats[:, 0] - row_max[None]), axis=0)
    log_total = row_max + jnp.log(row_sum)

    offsets = jnp.arange(queries_dev, dtype=jnp.int32)
    columns = jnp.arange(group_span, dtype=jnp.int32)
    positive = (columns[None, :] == (member_index * queries_dev + offsets)[:, None]).astype(
        jnp.float32
    )
    positive = positive[None] * own[:, None, None].astype(jnp.float32)
    factor = w_all * inverse_temp
    grad = (
        factor[:, :, None] * (jnp.exp(scores - log_total[:, :, None]) - positive)
    ).astype(jnp.bfloat16)

    delta_parts = jnp.einsum("gqk,ke->gqe", grad, group_codes, preferred_element_type=jnp.float32)
    returned = exchange(delta_parts.astype(jnp.bfloat16), "group").astype(jnp.float32)
    own_part = jnp.take(delta_parts, group_index, axis=0)
    query_delta = own_part + jnp.sum(jnp.where(own[:, None, None], 0.0, returned), axis=0)

    code_terms = None
    for g in range(groups):
        term = jnp.dot(grad[g].T, q_all[g], preferred_element_type=jnp.float32)
        term = jnp.where(g == group_index, term, term.astype(jnp.bfloat16).astype(jnp.float32))
        code_terms = term if code_terms is None else code_terms + term
    code_delta = lax.psum_scatter(
        code_terms.astype(jnp.bfloat16), "member", scatter_dimension=0, tiled=True
    ).astype(jnp.float32)

    dz_query = norm_back(query_delta, q_unit, q_inv)
    dz_code = norm_back(code_delta, c_unit, c_inv)
    query_grad = jnp.einsum(
        "qe,de->qd", dz_query, projection, preferred_element_type=jnp.float32
    ).astype(jnp.bfloat16)
    code_grad = jnp.einsum(
        "qe,de->qd", dz_code, projection, preferred_element_type=jnp.float32
    ).astype(jnp.bfloat16)

    dzq_all = shift_all(dz_query, "member")
    dzc_all = lax.all_gather(dz_code, "member", axis=0)
    proj_parts = jnp.einsum(
        "mqgr,mqe->gre", feat_cols[:, 0], dzq_all, preferred_element_type=jnp.float32
    ) + jnp.einsum("mqgr,mqe->gre", feat_cols[:, 1], dzc_all, preferred_element_type=jnp.float32)
    own_proj = jnp.take(proj_parts, group_index, axis=0)
    sent_proj = jnp.where(own[:, None, None], 0.0, proj_parts).astype(jnp.bfloat16)
    projection_grad = own_proj + lax.psum_scatter(
        sent_proj, "group", scatter_dimension=0, tiled=True
    ).reshape(rows_dev, emb_width).astype(jnp.float32)
    return (query_grad, code_grad, projection_grad)


def solution(mesh):
    return jax.shard_map(
        body,
        mesh=mesh,
        in_specs=(
            P(("group", "member"), None),
            P(("group", "member"), None),
            P(),
            P(("group", "member"), None),
            P(("group", "member")),
        ),
        out_specs=(
            P(("group", "member"), None),
            P(("group", "member"), None),
            P(("group", "member"), None),
        ),
        check_vma=False,
    )
```

```python
import jax
import jax.numpy as jnp
from jax import lax
from jax.sharding import PartitionSpec as P

CB = 64


inverse_temp = 120.0
epsilon = 1e-06


def embed(features, projection):
    values = jnp.dot(features, projection, preferred_element_type=jnp.float32)
    inverse = lax.rsqrt(jnp.sum(values * values, axis=1) + epsilon)
    unit_vec = values * inverse[:, None]
    return (unit_vec, inverse, unit_vec.astype(jnp.bfloat16))


def norm_back(upstream, unit_vec, inverse):
    inner_prod = jnp.sum(unit_vec * upstream, axis=1, keepdims=True)
    return (inverse[:, None] * (upstream - unit_vec * inner_prod)).astype(jnp.bfloat16)


def shift_all(x, axis):
    size = lax.axis_size(axis)
    index = lax.axis_index(axis)
    got = [x]
    for s in range(1, size):
        got.append(lax.ppermute(x, axis, [(i, (i + s) % size) for i in range(size)]))
    order = (index - jnp.arange(size)) % size
    return jax.tree.map(lambda *xs: jnp.take(jnp.stack(xs, axis=0), order, axis=0), *got)


def exchange(parts, axis):
    size = lax.axis_size(axis)
    index = lax.axis_index(axis)
    got = [jnp.take(parts, index, axis=0)]
    for s in range(1, size):
        sent = jnp.take(parts, (index + s) % size, axis=0)
        got.append(lax.ppermute(sent, axis, [(i, (i + s) % size) for i in range(size)]))
    stacked = jnp.stack(got, axis=0)
    return jnp.take(stacked, (index - jnp.arange(size)) % size, axis=0)


def body(query_feat, code_feat, projection, hard_ids, loss_weight):
    groups = lax.axis_size("group")
    members = lax.axis_size("member")
    group_index = lax.axis_index("group")
    member_index = lax.axis_index("member")
    queries_dev = query_feat.shape[0]
    feat_width = query_feat.shape[1]
    emb_width = projection.shape[1]
    slot_count = queries_dev // CB
    per_group = members * slot_count
    group_span = members * queries_dev
    rows_dev = feat_width // (groups * members)

    feats = jnp.stack([query_feat, code_feat], axis=0).reshape(
        2, queries_dev, groups, members, rows_dev
    )
    feats = jnp.transpose(feats, (3, 0, 1, 2, 4))
    feat_cols = exchange(feats, "member")

    q_unit, q_inv, q_emb = embed(query_feat, projection)
    c_unit, c_inv, c_emb = embed(code_feat, projection)
    group_codes = lax.all_gather(c_emb, "member", axis=0, tiled=True)
    q_all, ids_all, w_all = shift_all((q_emb, hard_ids[0], loss_weight), "group")

    block_ids = group_index * per_group + jnp.arange(per_group, dtype=jnp.int32)
    asked = jnp.any(ids_all[:, :, None] == block_ids[None, None, :], axis=1)
    own = jnp.arange(groups, dtype=jnp.int32) == group_index
    block_mask = asked | own[:, None]
    col_mask = jnp.broadcast_to(
        block_mask[:, :, None], (groups, per_group, CB)
    ).reshape(groups, 1, group_span)

    scores = inverse_temp * jnp.einsum(
        "gqe,ke->gqk", q_all, group_codes, preferred_element_type=jnp.float32
    )
    scores = jnp.where(col_mask, scores, -jnp.inf)
    part_max = jnp.max(scores, axis=2)
    safe_max = jnp.where(part_max > -jnp.inf, part_max, 0.0)
    part_sum = jnp.sum(jnp.exp(scores - safe_max[:, :, None]), axis=2)
    stats = shift_all(jnp.stack([part_max, part_sum], axis=0), "group")
    row_max = jnp.max(stats[:, 0], axis=0)
    row_sum = jnp.sum(stats[:, 1] * jnp.exp(stats[:, 0] - row_max[None]), axis=0)
    log_total = row_max + jnp.log(row_sum)

    offsets = jnp.arange(queries_dev, dtype=jnp.int32)
    columns = jnp.arange(group_span, dtype=jnp.int32)
    positive = (columns[None, :] == (member_index * queries_dev + offsets)[:, None]).astype(
        jnp.float32
    )
    positive = positive[None] * own[:, None, None].astype(jnp.float32)
    factor = w_all * inverse_temp
    grad = (
        factor[:, :, None] * (jnp.exp(scores - log_total[:, :, None]) - positive)
    ).astype(jnp.bfloat16)

    delta_parts = jnp.einsum("gqk,ke->gqe", grad, group_codes, preferred_element_type=jnp.float32)
    returned = exchange(delta_parts.astype(jnp.bfloat16), "group").astype(jnp.float32)
    own_part = jnp.take(delta_parts, group_index, axis=0)
    query_delta = own_part + jnp.sum(jnp.where(own[:, None, None], 0.0, returned), axis=0)

    code_terms = None
    for g in range(groups):
        term = jnp.dot(grad[g].T, q_all[g], preferred_element_type=jnp.float32)
        term = jnp.where(g == group_index, term, term.astype(jnp.bfloat16).astype(jnp.float32))
        code_terms = term if code_terms is None else code_terms + term
    code_delta = lax.psum_scatter(
        code_terms.astype(jnp.bfloat16), "member", scatter_dimension=0, tiled=True
    ).astype(jnp.float32)

    dz_query = norm_back(query_delta, q_unit, q_inv)
    dz_code = norm_back(code_delta, c_unit, c_inv)
    query_grad = jnp.einsum(
        "qe,de->qd", dz_query, projection, preferred_element_type=jnp.float32
    ).astype(jnp.bfloat16)
    code_grad = jnp.einsum(
        "qe,de->qd", dz_code, projection, preferred_element_type=jnp.float32
    ).astype(jnp.bfloat16)

    dz_all = lax.all_gather(jnp.stack([dz_query, dz_code], axis=0), "member", axis=0)
    proj_parts = jnp.einsum(
        "mtqgr,mtqe->gre", feat_cols, dz_all, preferred_element_type=jnp.float32
    )
    own_proj = jnp.take(proj_parts, group_index, axis=0)
    sent_proj = jnp.where(own[:, None, None], 0.0, proj_parts).astype(jnp.bfloat16)
    projection_grad = own_proj + lax.psum_scatter(
        sent_proj, "group", scatter_dimension=0, tiled=True
    ).reshape(rows_dev, emb_width).astype(jnp.float32)
    return (query_grad, code_grad, projection_grad)


def solution(mesh):
    return jax.shard_map(
        body,
        mesh=mesh,
        in_specs=(
            P(("group", "member"), None),
            P(("group", "member"), None),
            P(),
            P(("group", "member"), None),
            P(("group", "member")),
        ),
        out_specs=(
            P(("group", "member"), None),
            P(("group", "member"), None),
            P(("group", "member"), None),
        ),
        check_vma=False,
    )
```

```python
import jax
import jax.numpy as jnp
from jax import lax
from jax.sharding import PartitionSpec as P

CB = 64


inverse_temp = 120.0
epsilon = 1e-06


def embed(features, projection):
    values = jnp.dot(features, projection, preferred_element_type=jnp.float32)
    inverse = lax.rsqrt(jnp.sum(values * values, axis=1) + epsilon)
    unit_vec = values * inverse[:, None]
    return (unit_vec, inverse, unit_vec.astype(jnp.bfloat16))


def norm_back(upstream, unit_vec, inverse):
    inner_prod = jnp.sum(unit_vec * upstream, axis=1, keepdims=True)
    return (inverse[:, None] * (upstream - unit_vec * inner_prod)).astype(jnp.bfloat16)


def shift_all(x, axis):
    size = lax.axis_size(axis)
    index = lax.axis_index(axis)
    got = [x]
    for s in range(1, size):
        got.append(lax.ppermute(x, axis, [(i, (i + s) % size) for i in range(size)]))
    order = (index - jnp.arange(size)) % size
    return jax.tree.map(lambda *xs: jnp.take(jnp.stack(xs, axis=0), order, axis=0), *got)


def exchange(parts, axis):
    size = lax.axis_size(axis)
    index = lax.axis_index(axis)
    got = [jnp.take(parts, index, axis=0)]
    for s in range(1, size):
        sent = jnp.take(parts, (index + s) % size, axis=0)
        got.append(lax.ppermute(sent, axis, [(i, (i + s) % size) for i in range(size)]))
    stacked = jnp.stack(got, axis=0)
    return jnp.take(stacked, (index - jnp.arange(size)) % size, axis=0)


def body(query_feat, code_feat, projection, hard_ids, loss_weight):
    groups = lax.axis_size("group")
    members = lax.axis_size("member")
    group_index = lax.axis_index("group")
    member_index = lax.axis_index("member")
    queries_dev = query_feat.shape[0]
    feat_width = query_feat.shape[1]
    emb_width = projection.shape[1]
    slot_count = queries_dev // CB
    per_group = members * slot_count
    group_span = members * queries_dev
    rows_dev = feat_width // (groups * members)

    feats = jnp.stack([query_feat, code_feat], axis=0).reshape(
        2, queries_dev, groups, members, rows_dev
    )
    feats = jnp.transpose(feats, (3, 0, 1, 2, 4))
    feat_cols = lax.all_to_all(feats, "member", split_axis=0, concat_axis=0, tiled=True)

    q_unit, q_inv, q_emb = embed(query_feat, projection)
    c_unit, c_inv, c_emb = embed(code_feat, projection)
    group_codes = lax.all_gather(c_emb, "member", axis=0, tiled=True)
    q_all, ids_all, w_all = shift_all((q_emb, hard_ids[0], loss_weight), "group")

    block_ids = group_index * per_group + jnp.arange(per_group, dtype=jnp.int32)
    asked = jnp.any(ids_all[:, :, None] == block_ids[None, None, :], axis=1)
    own = jnp.arange(groups, dtype=jnp.int32) == group_index
    block_mask = asked | own[:, None]
    col_mask = jnp.broadcast_to(
        block_mask[:, :, None], (groups, per_group, CB)
    ).reshape(groups, 1, group_span)

    scores = inverse_temp * jnp.einsum(
        "gqe,ke->gqk", q_all, group_codes, preferred_element_type=jnp.float32
    )
    scores = jnp.where(col_mask, scores, -jnp.inf)
    part_max = jnp.max(scores, axis=2)
    safe_max = jnp.where(part_max > -jnp.inf, part_max, 0.0)
    part_sum = jnp.sum(jnp.exp(scores - safe_max[:, :, None]), axis=2)
    stats = shift_all(jnp.stack([part_max, part_sum], axis=0), "group")
    row_max = jnp.max(stats[:, 0], axis=0)
    row_sum = jnp.sum(stats[:, 1] * jnp.exp(stats[:, 0] - row_max[None]), axis=0)
    log_total = row_max + jnp.log(row_sum)

    offsets = jnp.arange(queries_dev, dtype=jnp.int32)
    columns = jnp.arange(group_span, dtype=jnp.int32)
    positive = (columns[None, :] == (member_index * queries_dev + offsets)[:, None]).astype(
        jnp.float32
    )
    positive = positive[None] * own[:, None, None].astype(jnp.float32)
    factor = w_all * inverse_temp
    grad = (
        factor[:, :, None] * (jnp.exp(scores - log_total[:, :, None]) - positive)
    ).astype(jnp.bfloat16)

    delta_parts = jnp.einsum("gqk,ke->gqe", grad, group_codes, preferred_element_type=jnp.float32)
    returned = exchange(delta_parts.astype(jnp.bfloat16), "group").astype(jnp.float32)
    own_part = jnp.take(delta_parts, group_index, axis=0)
    query_delta = own_part + jnp.sum(jnp.where(own[:, None, None], 0.0, returned), axis=0)

    code_terms = None
    for g in range(groups):
        term = jnp.dot(grad[g].T, q_all[g], preferred_element_type=jnp.float32)
        term = jnp.where(g == group_index, term, term.astype(jnp.bfloat16).astype(jnp.float32))
        code_terms = term if code_terms is None else code_terms + term
    code_delta = lax.psum_scatter(
        code_terms.astype(jnp.bfloat16), "member", scatter_dimension=0, tiled=True
    ).astype(jnp.float32)

    dz_query = norm_back(query_delta, q_unit, q_inv)
    dz_code = norm_back(code_delta, c_unit, c_inv)
    query_grad = jnp.einsum(
        "qe,de->qd", dz_query, projection, preferred_element_type=jnp.float32
    ).astype(jnp.bfloat16)
    code_grad = jnp.einsum(
        "qe,de->qd", dz_code, projection, preferred_element_type=jnp.float32
    ).astype(jnp.bfloat16)

    dz_all = lax.all_gather(jnp.stack([dz_query, dz_code], axis=0), "member", axis=0)
    proj_parts = jnp.einsum(
        "mtqgr,mtqe->gre", feat_cols, dz_all, preferred_element_type=jnp.float32
    )
    own_proj = jnp.take(proj_parts, group_index, axis=0)
    sent_proj = jnp.where(own[:, None, None], 0.0, proj_parts).astype(jnp.bfloat16)
    projection_grad = own_proj + lax.psum_scatter(
        sent_proj, "group", scatter_dimension=0, tiled=True
    ).reshape(rows_dev, emb_width).astype(jnp.float32)
    return (query_grad, code_grad, projection_grad)


def solution(mesh):
    return jax.shard_map(
        body,
        mesh=mesh,
        in_specs=(
            P(("group", "member"), None),
            P(("group", "member"), None),
            P(),
            P(("group", "member"), None),
            P(("group", "member")),
        ),
        out_specs=(
            P(("group", "member"), None),
            P(("group", "member"), None),
            P(("group", "member"), None),
        ),
        check_vma=False,
    )
```

```python
import jax
import jax.numpy as jnp
from jax import lax
from jax.sharding import PartitionSpec as P

CB = 64


inverse_temp = 120.0
epsilon = 1e-06


def embed(features, projection):
    values = jnp.dot(features, projection, preferred_element_type=jnp.float32)
    inverse = lax.rsqrt(jnp.sum(values * values, axis=1) + epsilon)
    unit_vec = values * inverse[:, None]
    return (unit_vec, inverse, unit_vec.astype(jnp.bfloat16))


def norm_back(upstream, unit_vec, inverse):
    inner_prod = jnp.sum(unit_vec * upstream, axis=1, keepdims=True)
    return (inverse[:, None] * (upstream - unit_vec * inner_prod)).astype(jnp.bfloat16)


def shift_all(x, axis):
    size = lax.axis_size(axis)
    index = lax.axis_index(axis)
    got = [x]
    for s in range(1, size):
        got.append(lax.ppermute(x, axis, [(i, (i + s) % size) for i in range(size)]))
    order = (index - jnp.arange(size)) % size
    return jax.tree.map(lambda *xs: jnp.take(jnp.stack(xs, axis=0), order, axis=0), *got)


def exchange(parts, axis):
    size = lax.axis_size(axis)
    index = lax.axis_index(axis)
    got = [jnp.take(parts, index, axis=0)]
    for s in range(1, size):
        sent = jnp.take(parts, (index + s) % size, axis=0)
        got.append(lax.ppermute(sent, axis, [(i, (i + s) % size) for i in range(size)]))
    stacked = jnp.stack(got, axis=0)
    return jnp.take(stacked, (index - jnp.arange(size)) % size, axis=0)


def body(query_feat, code_feat, projection, hard_ids, loss_weight):
    groups = lax.axis_size("group")
    members = lax.axis_size("member")
    group_index = lax.axis_index("group")
    member_index = lax.axis_index("member")
    queries_dev = query_feat.shape[0]
    feat_width = query_feat.shape[1]
    emb_width = projection.shape[1]
    slot_count = queries_dev // CB
    per_group = members * slot_count
    group_span = members * queries_dev
    rows_dev = feat_width // (groups * members)

    feats = jnp.stack([query_feat, code_feat], axis=0).reshape(
        2, queries_dev, groups, members, rows_dev
    )
    feats = jnp.transpose(feats, (3, 0, 1, 2, 4))
    feat_cols = lax.all_to_all(feats, "member", split_axis=0, concat_axis=0, tiled=True)

    q_unit, q_inv, q_emb = embed(query_feat, projection)
    c_unit, c_inv, c_emb = embed(code_feat, projection)
    group_codes = lax.all_gather(c_emb, "member", axis=0, tiled=True)
    q_all, ids_all, w_all = shift_all((q_emb, hard_ids[0], loss_weight), "group")

    block_ids = group_index * per_group + jnp.arange(per_group, dtype=jnp.int32)
    asked = jnp.any(ids_all[:, :, None] == block_ids[None, None, :], axis=1)
    own = jnp.arange(groups, dtype=jnp.int32) == group_index
    block_mask = asked | own[:, None]
    col_mask = jnp.broadcast_to(
        block_mask[:, :, None], (groups, per_group, CB)
    ).reshape(groups, 1, group_span)

    scores = inverse_temp * jnp.einsum(
        "gqe,ke->gqk", q_all, group_codes, preferred_element_type=jnp.float32
    )
    scores = jnp.where(col_mask, scores, -jnp.inf)
    part_max = jnp.max(scores, axis=2)
    safe_max = jnp.where(part_max > -jnp.inf, part_max, 0.0)
    part_sum = jnp.sum(jnp.exp(scores - safe_max[:, :, None]), axis=2)
    stats = shift_all(jnp.stack([part_max, part_sum], axis=0), "group")
    row_max = jnp.max(stats[:, 0], axis=0)
    row_sum = jnp.sum(stats[:, 1] * jnp.exp(stats[:, 0] - row_max[None]), axis=0)
    log_total = row_max + jnp.log(row_sum)

    offsets = jnp.arange(queries_dev, dtype=jnp.int32)
    columns = jnp.arange(group_span, dtype=jnp.int32)
    positive = (columns[None, :] == (member_index * queries_dev + offsets)[:, None]).astype(
        jnp.float32
    )
    positive = positive[None] * own[:, None, None].astype(jnp.float32)
    factor = w_all * inverse_temp
    grad = (
        factor[:, :, None] * (jnp.exp(scores - log_total[:, :, None]) - positive)
    ).astype(jnp.bfloat16)

    delta_parts = jnp.einsum("gqk,ke->gqe", grad, group_codes, preferred_element_type=jnp.float32)
    returned = exchange(delta_parts.astype(jnp.bfloat16), "group").astype(jnp.float32)
    own_part = jnp.take(delta_parts, group_index, axis=0)
    query_delta = own_part + jnp.sum(jnp.where(own[:, None, None], 0.0, returned), axis=0)

    code_terms = None
    for g in range(groups):
        term = jnp.dot(grad[g].T, q_all[g], preferred_element_type=jnp.float32)
        term = jnp.where(g == group_index, term, term.astype(jnp.bfloat16).astype(jnp.float32))
        code_terms = term if code_terms is None else code_terms + term
    halves = code_terms.astype(jnp.bfloat16).reshape(members, 2, queries_dev // 2, emb_width)
    first_half = lax.psum_scatter(
        halves[:, 0].reshape(members * queries_dev // 2, emb_width),
        "member",
        scatter_dimension=0,
        tiled=True,
    ).astype(jnp.float32)
    second_half = jnp.sum(
        lax.all_to_all(halves[:, 1], "member", split_axis=0, concat_axis=0, tiled=True).astype(
            jnp.float32
        ),
        axis=0,
    )
    code_delta = jnp.concatenate([first_half, second_half], axis=0)

    dz_query = norm_back(query_delta, q_unit, q_inv)
    dz_code = norm_back(code_delta, c_unit, c_inv)
    query_grad = jnp.einsum(
        "qe,de->qd", dz_query, projection, preferred_element_type=jnp.float32
    ).astype(jnp.bfloat16)
    code_grad = jnp.einsum(
        "qe,de->qd", dz_code, projection, preferred_element_type=jnp.float32
    ).astype(jnp.bfloat16)

    dz_all = lax.all_gather(jnp.stack([dz_query, dz_code], axis=0), "member", axis=0)
    proj_parts = jnp.einsum(
        "mtqgr,mtqe->gre", feat_cols, dz_all, preferred_element_type=jnp.float32
    )
    own_proj = jnp.take(proj_parts, group_index, axis=0)
    sent_proj = jnp.where(own[:, None, None], 0.0, proj_parts).astype(jnp.bfloat16)
    projection_grad = own_proj + lax.psum_scatter(
        sent_proj, "group", scatter_dimension=0, tiled=True
    ).reshape(rows_dev, emb_width).astype(jnp.float32)
    return (query_grad, code_grad, projection_grad)


def solution(mesh):
    return jax.shard_map(
        body,
        mesh=mesh,
        in_specs=(
            P(("group", "member"), None),
            P(("group", "member"), None),
            P(),
            P(("group", "member"), None),
            P(("group", "member")),
        ),
        out_specs=(
            P(("group", "member"), None),
            P(("group", "member"), None),
            P(("group", "member"), None),
        ),
        check_vma=False,
    )
```

```python
import jax
import jax.numpy as jnp
from jax import lax
from jax.sharding import PartitionSpec as P

CB = 64


inverse_temp = 120.0
epsilon = 1e-06


def embed(features, projection):
    values = jnp.dot(features, projection, preferred_element_type=jnp.float32)
    inverse = lax.rsqrt(jnp.sum(values * values, axis=1) + epsilon)
    unit_vec = values * inverse[:, None]
    return (unit_vec, inverse, unit_vec.astype(jnp.bfloat16))


def norm_back(upstream, unit_vec, inverse):
    inner_prod = jnp.sum(unit_vec * upstream, axis=1, keepdims=True)
    return (inverse[:, None] * (upstream - unit_vec * inner_prod)).astype(jnp.bfloat16)


def shift_all(x, axis):
    size = lax.axis_size(axis)
    index = lax.axis_index(axis)
    got = [x]
    for s in range(1, size):
        got.append(lax.ppermute(x, axis, [(i, (i + s) % size) for i in range(size)]))
    order = (index - jnp.arange(size)) % size
    return jax.tree.map(lambda *xs: jnp.take(jnp.stack(xs, axis=0), order, axis=0), *got)


def exchange(parts, axis):
    size = lax.axis_size(axis)
    index = lax.axis_index(axis)
    got = [jnp.take(parts, index, axis=0)]
    for s in range(1, size):
        sent = jnp.take(parts, (index + s) % size, axis=0)
        got.append(lax.ppermute(sent, axis, [(i, (i + s) % size) for i in range(size)]))
    stacked = jnp.stack(got, axis=0)
    return jnp.take(stacked, (index - jnp.arange(size)) % size, axis=0)


def body(query_feat, code_feat, projection, hard_ids, loss_weight):
    groups = lax.axis_size("group")
    members = lax.axis_size("member")
    group_index = lax.axis_index("group")
    member_index = lax.axis_index("member")
    queries_dev = query_feat.shape[0]
    feat_width = query_feat.shape[1]
    emb_width = projection.shape[1]
    slot_count = queries_dev // CB
    per_group = members * slot_count
    group_span = members * queries_dev
    rows_dev = feat_width // (groups * members)

    feats = jnp.stack([query_feat, code_feat], axis=0).reshape(
        2, queries_dev, groups, members, rows_dev
    )
    feats = jnp.transpose(feats, (3, 0, 1, 2, 4))
    feat_cols = lax.all_to_all(feats, "member", split_axis=0, concat_axis=0, tiled=True)

    q_unit, q_inv, q_emb = embed(query_feat, projection)
    c_unit, c_inv, c_emb = embed(code_feat, projection)
    group_codes = lax.all_gather(c_emb, "member", axis=0, tiled=True)
    q_all, ids_all, w_all = shift_all((q_emb, hard_ids[0], loss_weight), "group")

    block_ids = group_index * per_group + jnp.arange(per_group, dtype=jnp.int32)
    asked = jnp.any(ids_all[:, :, None] == block_ids[None, None, :], axis=1)
    own = jnp.arange(groups, dtype=jnp.int32) == group_index
    block_mask = asked | own[:, None]
    col_mask = jnp.broadcast_to(
        block_mask[:, :, None], (groups, per_group, CB)
    ).reshape(groups, 1, group_span)

    scores = inverse_temp * jnp.einsum(
        "gqe,ke->gqk", q_all, group_codes, preferred_element_type=jnp.float32
    )
    scores = jnp.where(col_mask, scores, -jnp.inf)
    part_max = jnp.max(scores, axis=2)
    safe_max = jnp.where(part_max > -jnp.inf, part_max, 0.0)
    part_sum = jnp.sum(jnp.exp(scores - safe_max[:, :, None]), axis=2)
    stats = shift_all(jnp.stack([part_max, part_sum], axis=0), "group")
    row_max = jnp.max(stats[:, 0], axis=0)
    row_sum = jnp.sum(stats[:, 1] * jnp.exp(stats[:, 0] - row_max[None]), axis=0)
    log_total = row_max + jnp.log(row_sum)

    offsets = jnp.arange(queries_dev, dtype=jnp.int32)
    columns = jnp.arange(group_span, dtype=jnp.int32)
    positive = (columns[None, :] == (member_index * queries_dev + offsets)[:, None]).astype(
        jnp.float32
    )
    positive = positive[None] * own[:, None, None].astype(jnp.float32)
    factor = w_all * inverse_temp
    grad = (
        factor[:, :, None] * (jnp.exp(scores - log_total[:, :, None]) - positive)
    ).astype(jnp.bfloat16)

    delta_parts = jnp.einsum("gqk,ke->gqe", grad, group_codes, preferred_element_type=jnp.float32)
    returned = exchange(delta_parts.astype(jnp.bfloat16), "group").astype(jnp.float32)
    own_part = jnp.take(delta_parts, group_index, axis=0)
    query_delta = own_part + jnp.sum(jnp.where(own[:, None, None], 0.0, returned), axis=0)

    code_terms = None
    for g in range(groups):
        term = jnp.dot(grad[g].T, q_all[g], preferred_element_type=jnp.float32)
        term = jnp.where(g == group_index, term, term.astype(jnp.bfloat16).astype(jnp.float32))
        code_terms = term if code_terms is None else code_terms + term
    code_delta = jnp.sum(
        lax.all_to_all(
            code_terms.astype(jnp.bfloat16).reshape(members, queries_dev, emb_width),
            "member",
            split_axis=0,
            concat_axis=0,
            tiled=True,
        ).astype(jnp.float32),
        axis=0,
    )

    dz_query = norm_back(query_delta, q_unit, q_inv)
    dz_code = norm_back(code_delta, c_unit, c_inv)
    query_grad = jnp.einsum(
        "qe,de->qd", dz_query, projection, preferred_element_type=jnp.float32
    ).astype(jnp.bfloat16)
    code_grad = jnp.einsum(
        "qe,de->qd", dz_code, projection, preferred_element_type=jnp.float32
    ).astype(jnp.bfloat16)

    dzq_all = lax.all_to_all(
        jnp.broadcast_to(dz_query[None], (members, queries_dev, emb_width)),
        "member",
        split_axis=0,
        concat_axis=0,
        tiled=True,
    )
    dzc_all = lax.all_gather(dz_code, "member", axis=0)
    proj_parts = jnp.einsum(
        "mqgr,mqe->gre", feat_cols[:, 0], dzq_all, preferred_element_type=jnp.float32
    ) + jnp.einsum("mqgr,mqe->gre", feat_cols[:, 1], dzc_all, preferred_element_type=jnp.float32)
    own_proj = jnp.take(proj_parts, group_index, axis=0)
    sent_proj = jnp.where(own[:, None, None], 0.0, proj_parts).astype(jnp.bfloat16)
    projection_grad = own_proj + lax.psum_scatter(
        sent_proj, "group", scatter_dimension=0, tiled=True
    ).reshape(rows_dev, emb_width).astype(jnp.float32)
    return (query_grad, code_grad, projection_grad)


def solution(mesh):
    return jax.shard_map(
        body,
        mesh=mesh,
        in_specs=(
            P(("group", "member"), None),
            P(("group", "member"), None),
            P(),
            P(("group", "member"), None),
            P(("group", "member")),
        ),
        out_specs=(
            P(("group", "member"), None),
            P(("group", "member"), None),
            P(("group", "member"), None),
        ),
        check_vma=False,
    )
```

```python
import jax
import jax.numpy as jnp
from jax import lax
from jax.sharding import PartitionSpec as P

CB = 64


inverse_temp = 120.0
epsilon = 1e-06


def embed(features, projection):
    values = jnp.dot(features, projection, preferred_element_type=jnp.float32)
    inverse = lax.rsqrt(jnp.sum(values * values, axis=1) + epsilon)
    unit_vec = values * inverse[:, None]
    return (unit_vec, inverse, unit_vec.astype(jnp.bfloat16))


def norm_back(upstream, unit_vec, inverse):
    inner_prod = jnp.sum(unit_vec * upstream, axis=1, keepdims=True)
    return (inverse[:, None] * (upstream - unit_vec * inner_prod)).astype(jnp.bfloat16)


def shift_all(x, axis):
    size = lax.axis_size(axis)
    index = lax.axis_index(axis)
    got = [x]
    for s in range(1, size):
        got.append(lax.ppermute(x, axis, [(i, (i + s) % size) for i in range(size)]))
    order = (index - jnp.arange(size)) % size
    return jax.tree.map(lambda *xs: jnp.take(jnp.stack(xs, axis=0), order, axis=0), *got)


def exchange(parts, axis):
    size = lax.axis_size(axis)
    index = lax.axis_index(axis)
    got = [jnp.take(parts, index, axis=0)]
    for s in range(1, size):
        sent = jnp.take(parts, (index + s) % size, axis=0)
        got.append(lax.ppermute(sent, axis, [(i, (i + s) % size) for i in range(size)]))
    stacked = jnp.stack(got, axis=0)
    return jnp.take(stacked, (index - jnp.arange(size)) % size, axis=0)


def body(query_feat, code_feat, projection, hard_ids, loss_weight):
    groups = lax.axis_size("group")
    members = lax.axis_size("member")
    group_index = lax.axis_index("group")
    member_index = lax.axis_index("member")
    queries_dev = query_feat.shape[0]
    feat_width = query_feat.shape[1]
    emb_width = projection.shape[1]
    slot_count = queries_dev // CB
    per_group = members * slot_count
    group_span = members * queries_dev
    rows_dev = feat_width // (groups * members)

    feats = jnp.stack([query_feat, code_feat], axis=0).reshape(
        2, queries_dev, groups, members, rows_dev
    )
    feats = jnp.transpose(feats, (3, 0, 1, 2, 4))
    feat_cols = lax.all_to_all(feats, "member", split_axis=0, concat_axis=0, tiled=True)

    q_unit, q_inv, q_emb = embed(query_feat, projection)
    c_unit, c_inv, c_emb = embed(code_feat, projection)
    group_codes = lax.all_gather(c_emb, "member", axis=0, tiled=True)
    q_all = lax.all_to_all(
        jnp.broadcast_to(q_emb[None], (groups, queries_dev, emb_width)),
        "group",
        split_axis=0,
        concat_axis=0,
        tiled=True,
    )
    ids_all = shift_all(hard_ids[0], "group")

    block_ids = group_index * per_group + jnp.arange(per_group, dtype=jnp.int32)
    asked = jnp.any(ids_all[:, :, None] == block_ids[None, None, :], axis=1)
    own = jnp.arange(groups, dtype=jnp.int32) == group_index
    block_mask = asked | own[:, None]
    col_mask = jnp.broadcast_to(
        block_mask[:, :, None], (groups, per_group, CB)
    ).reshape(groups, 1, group_span)

    scores = inverse_temp * jnp.einsum(
        "gqe,ke->gqk", q_all, group_codes, preferred_element_type=jnp.float32
    )
    scores = jnp.where(col_mask, scores, -jnp.inf)
    part_max = jnp.max(scores, axis=2)
    safe_max = jnp.where(part_max > -jnp.inf, part_max, 0.0)
    part_sum = jnp.sum(jnp.exp(scores - safe_max[:, :, None]), axis=2)
    weights_row = jnp.broadcast_to(loss_weight[None], (groups, queries_dev))
    stats = shift_all(jnp.stack([part_max, part_sum, weights_row], axis=0), "group")
    w_all = stats[:, 2, 0]
    row_max = jnp.max(stats[:, 0], axis=0)
    row_sum = jnp.sum(stats[:, 1] * jnp.exp(stats[:, 0] - row_max[None]), axis=0)
    log_total = row_max + jnp.log(row_sum)

    offsets = jnp.arange(queries_dev, dtype=jnp.int32)
    columns = jnp.arange(group_span, dtype=jnp.int32)
    positive = (columns[None, :] == (member_index * queries_dev + offsets)[:, None]).astype(
        jnp.float32
    )
    positive = positive[None] * own[:, None, None].astype(jnp.float32)
    factor = w_all * inverse_temp
    grad = (
        factor[:, :, None] * (jnp.exp(scores - log_total[:, :, None]) - positive)
    ).astype(jnp.bfloat16)

    delta_parts = jnp.einsum("gqk,ke->gqe", grad, group_codes, preferred_element_type=jnp.float32)
    returned = exchange(delta_parts.astype(jnp.bfloat16), "group").astype(jnp.float32)
    own_part = jnp.take(delta_parts, group_index, axis=0)
    query_delta = own_part + jnp.sum(jnp.where(own[:, None, None], 0.0, returned), axis=0)

    code_terms = None
    for g in range(groups):
        term = jnp.dot(grad[g].T, q_all[g], preferred_element_type=jnp.float32)
        term = jnp.where(g == group_index, term, term.astype(jnp.bfloat16).astype(jnp.float32))
        code_terms = term if code_terms is None else code_terms + term
    halves = code_terms.astype(jnp.bfloat16).reshape(members, 2, queries_dev // 2, emb_width)
    first_half = lax.psum_scatter(
        halves[:, 0].reshape(members * queries_dev // 2, emb_width),
        "member",
        scatter_dimension=0,
        tiled=True,
    ).astype(jnp.float32)
    second_half = jnp.sum(
        lax.all_to_all(halves[:, 1], "member", split_axis=0, concat_axis=0, tiled=True).astype(
            jnp.float32
        ),
        axis=0,
    )
    code_delta = jnp.concatenate([first_half, second_half], axis=0)

    dz_query = norm_back(query_delta, q_unit, q_inv)
    dz_code = norm_back(code_delta, c_unit, c_inv)
    query_grad = jnp.einsum(
        "qe,de->qd", dz_query, projection, preferred_element_type=jnp.float32
    ).astype(jnp.bfloat16)
    code_grad = jnp.einsum(
        "qe,de->qd", dz_code, projection, preferred_element_type=jnp.float32
    ).astype(jnp.bfloat16)

    dz_all = lax.all_gather(jnp.stack([dz_query, dz_code], axis=0), "member", axis=0)
    proj_parts = jnp.einsum(
        "mtqgr,mtqe->gre", feat_cols, dz_all, preferred_element_type=jnp.float32
    )
    own_proj = jnp.take(proj_parts, group_index, axis=0)
    sent_proj = jnp.where(own[:, None, None], 0.0, proj_parts).astype(jnp.bfloat16)
    projection_grad = own_proj + lax.psum_scatter(
        sent_proj, "group", scatter_dimension=0, tiled=True
    ).reshape(rows_dev, emb_width).astype(jnp.float32)
    return (query_grad, code_grad, projection_grad)


def solution(mesh):
    return jax.shard_map(
        body,
        mesh=mesh,
        in_specs=(
            P(("group", "member"), None),
            P(("group", "member"), None),
            P(),
            P(("group", "member"), None),
            P(("group", "member")),
        ),
        out_specs=(
            P(("group", "member"), None),
            P(("group", "member"), None),
            P(("group", "member"), None),
        ),
        check_vma=False,
    )
```

```python
import jax
import jax.numpy as jnp
from jax import lax
from jax.sharding import PartitionSpec as P

CB = 64


inverse_temp = 120.0
epsilon = 1e-06


def embed(features, projection):
    values = jnp.dot(features, projection, preferred_element_type=jnp.float32)
    inverse = lax.rsqrt(jnp.sum(values * values, axis=1) + epsilon)
    unit_vec = values * inverse[:, None]
    return (unit_vec, inverse, unit_vec.astype(jnp.bfloat16))


def norm_back(upstream, unit_vec, inverse):
    inner_prod = jnp.sum(unit_vec * upstream, axis=1, keepdims=True)
    return (inverse[:, None] * (upstream - unit_vec * inner_prod)).astype(jnp.bfloat16)


def shift_all(x, axis):
    size = lax.axis_size(axis)
    index = lax.axis_index(axis)
    got = [x]
    for s in range(1, size):
        got.append(lax.ppermute(x, axis, [(i, (i + s) % size) for i in range(size)]))
    order = (index - jnp.arange(size)) % size
    return jax.tree.map(lambda *xs: jnp.take(jnp.stack(xs, axis=0), order, axis=0), *got)


def exchange(parts, axis):
    size = lax.axis_size(axis)
    index = lax.axis_index(axis)
    got = [jnp.take(parts, index, axis=0)]
    for s in range(1, size):
        sent = jnp.take(parts, (index + s) % size, axis=0)
        got.append(lax.ppermute(sent, axis, [(i, (i + s) % size) for i in range(size)]))
    stacked = jnp.stack(got, axis=0)
    return jnp.take(stacked, (index - jnp.arange(size)) % size, axis=0)


def body(query_feat, code_feat, projection, hard_ids, loss_weight):
    groups = lax.axis_size("group")
    members = lax.axis_size("member")
    group_index = lax.axis_index("group")
    member_index = lax.axis_index("member")
    queries_dev = query_feat.shape[0]
    feat_width = query_feat.shape[1]
    emb_width = projection.shape[1]
    slot_count = queries_dev // CB
    per_group = members * slot_count
    group_span = members * queries_dev
    rows_dev = feat_width // (groups * members)

    feats = jnp.stack([query_feat, code_feat], axis=0).reshape(
        2, queries_dev, groups, members, rows_dev
    )
    feats = jnp.transpose(feats, (3, 0, 1, 2, 4))
    feat_cols = lax.all_to_all(feats, "member", split_axis=0, concat_axis=0, tiled=True)

    q_unit, q_inv, q_emb = embed(query_feat, projection)
    code_values = lax.all_gather(
        jnp.dot(code_feat, projection, preferred_element_type=jnp.float32),
        "member",
        axis=0,
        tiled=True,
    )
    c_inv = lax.rsqrt(jnp.sum(code_values * code_values, axis=1) + epsilon)
    c_unit = code_values * c_inv[:, None]
    group_codes = c_unit.astype(jnp.bfloat16)
    q_all = lax.all_to_all(
        jnp.broadcast_to(q_emb[None], (groups, queries_dev, emb_width)),
        "group",
        split_axis=0,
        concat_axis=0,
        tiled=True,
    )
    ids_all = shift_all(hard_ids[0], "group")

    block_ids = group_index * per_group + jnp.arange(per_group, dtype=jnp.int32)
    asked = jnp.any(ids_all[:, :, None] == block_ids[None, None, :], axis=1)
    own = jnp.arange(groups, dtype=jnp.int32) == group_index
    block_mask = asked | own[:, None]
    col_mask = jnp.broadcast_to(
        block_mask[:, :, None], (groups, per_group, CB)
    ).reshape(groups, 1, group_span)

    scores = inverse_temp * jnp.einsum(
        "gqe,ke->gqk", q_all, group_codes, preferred_element_type=jnp.float32
    )
    scores = jnp.where(col_mask, scores, -jnp.inf)
    part_max = jnp.max(scores, axis=2)
    safe_max = jnp.where(part_max > -jnp.inf, part_max, 0.0)
    part_sum = jnp.sum(jnp.exp(scores - safe_max[:, :, None]), axis=2)
    weights_row = jnp.broadcast_to(loss_weight[None], (groups, queries_dev))
    stats = shift_all(jnp.stack([part_max, part_sum, weights_row], axis=0), "group")
    w_all = stats[:, 2, 0]
    row_max = jnp.max(stats[:, 0], axis=0)
    row_sum = jnp.sum(stats[:, 1] * jnp.exp(stats[:, 0] - row_max[None]), axis=0)
    log_total = row_max + jnp.log(row_sum)

    offsets = jnp.arange(queries_dev, dtype=jnp.int32)
    columns = jnp.arange(group_span, dtype=jnp.int32)
    positive = (columns[None, :] == (member_index * queries_dev + offsets)[:, None]).astype(
        jnp.float32
    )
    positive = positive[None] * own[:, None, None].astype(jnp.float32)
    factor = w_all * inverse_temp
    grad = (
        factor[:, :, None] * (jnp.exp(scores - log_total[:, :, None]) - positive)
    ).astype(jnp.bfloat16)

    delta_parts = jnp.einsum("gqk,ke->gqe", grad, group_codes, preferred_element_type=jnp.float32)
    returned = exchange(delta_parts.astype(jnp.bfloat16), "group").astype(jnp.float32)
    own_part = jnp.take(delta_parts, group_index, axis=0)
    query_delta = own_part + jnp.sum(jnp.where(own[:, None, None], 0.0, returned), axis=0)

    code_terms = None
    for g in range(groups):
        term = jnp.dot(grad[g].T, q_all[g], preferred_element_type=jnp.float32)
        term = jnp.where(g == group_index, term, term.astype(jnp.bfloat16).astype(jnp.float32))
        code_terms = term if code_terms is None else code_terms + term
    code_delta = lax.psum(code_terms.astype(jnp.bfloat16), "member").astype(jnp.float32)

    dz_query = norm_back(query_delta, q_unit, q_inv)
    dz_code_all = norm_back(code_delta, c_unit, c_inv)
    dz_code = lax.dynamic_slice_in_dim(dz_code_all, member_index * queries_dev, queries_dev, 0)
    query_grad = jnp.einsum(
        "qe,de->qd", dz_query, projection, preferred_element_type=jnp.float32
    ).astype(jnp.bfloat16)
    code_grad = jnp.einsum(
        "qe,de->qd", dz_code, projection, preferred_element_type=jnp.float32
    ).astype(jnp.bfloat16)

    dzq_all = lax.all_to_all(
        jnp.broadcast_to(dz_query[None], (members, queries_dev, emb_width)),
        "member",
        split_axis=0,
        concat_axis=0,
        tiled=True,
    )
    dzc_all = dz_code_all.reshape(members, queries_dev, emb_width)
    proj_parts = jnp.einsum(
        "mqgr,mqe->gre", feat_cols[:, 0], dzq_all, preferred_element_type=jnp.float32
    ) + jnp.einsum("mqgr,mqe->gre", feat_cols[:, 1], dzc_all, preferred_element_type=jnp.float32)
    own_proj = jnp.take(proj_parts, group_index, axis=0)
    sent_proj = jnp.where(own[:, None, None], 0.0, proj_parts).astype(jnp.bfloat16)
    projection_grad = own_proj + lax.psum_scatter(
        sent_proj, "group", scatter_dimension=0, tiled=True
    ).reshape(rows_dev, emb_width).astype(jnp.float32)
    return (query_grad, code_grad, projection_grad)


def solution(mesh):
    return jax.shard_map(
        body,
        mesh=mesh,
        in_specs=(
            P(("group", "member"), None),
            P(("group", "member"), None),
            P(),
            P(("group", "member"), None),
            P(("group", "member")),
        ),
        out_specs=(
            P(("group", "member"), None),
            P(("group", "member"), None),
            P(("group", "member"), None),
        ),
        check_vma=False,
    )
```

```python
import jax
import jax.numpy as jnp
from jax import lax
from jax.sharding import PartitionSpec as P

CB = 64


inverse_temp = 120.0
epsilon = 1e-06


def embed(features, projection):
    values = jnp.dot(features, projection, preferred_element_type=jnp.float32)
    inverse = lax.rsqrt(jnp.sum(values * values, axis=1) + epsilon)
    unit_vec = values * inverse[:, None]
    return (unit_vec, inverse, unit_vec.astype(jnp.bfloat16))


def norm_back(upstream, unit_vec, inverse):
    inner_prod = jnp.sum(unit_vec * upstream, axis=1, keepdims=True)
    return (inverse[:, None] * (upstream - unit_vec * inner_prod)).astype(jnp.bfloat16)


def shift_all(x, axis):
    size = lax.axis_size(axis)
    index = lax.axis_index(axis)
    got = [x]
    for s in range(1, size):
        got.append(lax.ppermute(x, axis, [(i, (i + s) % size) for i in range(size)]))
    order = (index - jnp.arange(size)) % size
    return jax.tree.map(lambda *xs: jnp.take(jnp.stack(xs, axis=0), order, axis=0), *got)


def exchange(parts, axis):
    size = lax.axis_size(axis)
    index = lax.axis_index(axis)
    got = [jnp.take(parts, index, axis=0)]
    for s in range(1, size):
        sent = jnp.take(parts, (index + s) % size, axis=0)
        got.append(lax.ppermute(sent, axis, [(i, (i + s) % size) for i in range(size)]))
    stacked = jnp.stack(got, axis=0)
    return jnp.take(stacked, (index - jnp.arange(size)) % size, axis=0)


def body(query_feat, code_feat, projection, hard_ids, loss_weight):
    groups = lax.axis_size("group")
    members = lax.axis_size("member")
    group_index = lax.axis_index("group")
    member_index = lax.axis_index("member")
    queries_dev = query_feat.shape[0]
    feat_width = query_feat.shape[1]
    emb_width = projection.shape[1]
    slot_count = queries_dev // CB
    per_group = members * slot_count
    group_span = members * queries_dev
    rows_dev = feat_width // (groups * members)

    feats = jnp.stack([query_feat, code_feat], axis=0).reshape(
        2, queries_dev, groups, members, rows_dev
    )
    feats = jnp.transpose(feats, (3, 0, 1, 2, 4))

    q_unit, q_inv, q_emb = embed(query_feat, projection)
    code_values = lax.all_gather(
        jnp.dot(code_feat, projection, preferred_element_type=jnp.float32),
        "member",
        axis=0,
        tiled=True,
    )
    c_inv = lax.rsqrt(jnp.sum(code_values * code_values, axis=1) + epsilon)
    c_unit = code_values * c_inv[:, None]
    group_codes = c_unit.astype(jnp.bfloat16)
    q_all = lax.all_to_all(
        jnp.broadcast_to(q_emb[None], (groups, queries_dev, emb_width)),
        "group",
        split_axis=0,
        concat_axis=0,
        tiled=True,
    )
    ids_all = shift_all(hard_ids[0], "group")

    block_ids = group_index * per_group + jnp.arange(per_group, dtype=jnp.int32)
    asked = jnp.any(ids_all[:, :, None] == block_ids[None, None, :], axis=1)
    own = jnp.arange(groups, dtype=jnp.int32) == group_index
    block_mask = asked | own[:, None]
    col_mask = jnp.broadcast_to(
        block_mask[:, :, None], (groups, per_group, CB)
    ).reshape(groups, 1, group_span)

    scores = inverse_temp * jnp.einsum(
        "gqe,ke->gqk", q_all, group_codes, preferred_element_type=jnp.float32
    )
    scores = jnp.where(col_mask, scores, -jnp.inf)
    part_max = jnp.max(scores, axis=2)
    safe_max = jnp.where(part_max > -jnp.inf, part_max, 0.0)
    part_sum = jnp.sum(jnp.exp(scores - safe_max[:, :, None]), axis=2)
    weights_row = jnp.broadcast_to(loss_weight[None], (groups, queries_dev))
    stats = shift_all(jnp.stack([part_max, part_sum, weights_row], axis=0), "group")
    w_all = stats[:, 2, 0]
    row_max = jnp.max(stats[:, 0], axis=0)
    row_sum = jnp.sum(stats[:, 1] * jnp.exp(stats[:, 0] - row_max[None]), axis=0)
    log_total = row_max + jnp.log(row_sum)

    offsets = jnp.arange(queries_dev, dtype=jnp.int32)
    columns = jnp.arange(group_span, dtype=jnp.int32)
    positive = (columns[None, :] == (member_index * queries_dev + offsets)[:, None]).astype(
        jnp.float32
    )
    positive = positive[None] * own[:, None, None].astype(jnp.float32)
    factor = w_all * inverse_temp
    grad = (
        factor[:, :, None] * (jnp.exp(scores - log_total[:, :, None]) - positive)
    ).astype(jnp.bfloat16)

    delta_parts = jnp.einsum("gqk,ke->gqe", grad, group_codes, preferred_element_type=jnp.float32)
    returned = exchange(delta_parts.astype(jnp.bfloat16), "group").astype(jnp.float32)
    feats, returned = lax.optimization_barrier((feats, returned))
    feat_cols = lax.all_to_all(feats, "member", split_axis=0, concat_axis=0, tiled=True)
    own_part = jnp.take(delta_parts, group_index, axis=0)
    query_delta = own_part + jnp.sum(jnp.where(own[:, None, None], 0.0, returned), axis=0)

    code_terms = None
    for g in range(groups):
        term = jnp.dot(grad[g].T, q_all[g], preferred_element_type=jnp.float32)
        term = jnp.where(g == group_index, term, term.astype(jnp.bfloat16).astype(jnp.float32))
        code_terms = term if code_terms is None else code_terms + term
    code_delta = lax.psum(code_terms.astype(jnp.bfloat16), "member").astype(jnp.float32)

    dz_query = norm_back(query_delta, q_unit, q_inv)
    dz_code_all = norm_back(code_delta, c_unit, c_inv)
    dz_code = lax.dynamic_slice_in_dim(dz_code_all, member_index * queries_dev, queries_dev, 0)
    query_grad = jnp.einsum(
        "qe,de->qd", dz_query, projection, preferred_element_type=jnp.float32
    ).astype(jnp.bfloat16)
    code_grad = jnp.einsum(
        "qe,de->qd", dz_code, projection, preferred_element_type=jnp.float32
    ).astype(jnp.bfloat16)

    dzq_all = lax.all_to_all(
        jnp.broadcast_to(dz_query[None], (members, queries_dev, emb_width)),
        "member",
        split_axis=0,
        concat_axis=0,
        tiled=True,
    )
    dzc_all = dz_code_all.reshape(members, queries_dev, emb_width)
    proj_parts = jnp.einsum(
        "mqgr,mqe->gre", feat_cols[:, 0], dzq_all, preferred_element_type=jnp.float32
    ) + jnp.einsum("mqgr,mqe->gre", feat_cols[:, 1], dzc_all, preferred_element_type=jnp.float32)
    own_proj = jnp.take(proj_parts, group_index, axis=0)
    sent_proj = jnp.where(own[:, None, None], 0.0, proj_parts).astype(jnp.bfloat16)
    projection_grad = own_proj + lax.psum_scatter(
        sent_proj, "group", scatter_dimension=0, tiled=True
    ).reshape(rows_dev, emb_width).astype(jnp.float32)
    return (query_grad, code_grad, projection_grad)


def solution(mesh):
    return jax.shard_map(
        body,
        mesh=mesh,
        in_specs=(
            P(("group", "member"), None),
            P(("group", "member"), None),
            P(),
            P(("group", "member"), None),
            P(("group", "member")),
        ),
        out_specs=(
            P(("group", "member"), None),
            P(("group", "member"), None),
            P(("group", "member"), None),
        ),
        check_vma=False,
    )
```

```python
import jax
import jax.numpy as jnp
from jax import lax
from jax.sharding import PartitionSpec as P

CB = 64


inverse_temp = 120.0
epsilon = 1e-06


def embed(features, projection):
    values = jnp.dot(features, projection, preferred_element_type=jnp.float32)
    inverse = lax.rsqrt(jnp.sum(values * values, axis=1) + epsilon)
    unit_vec = values * inverse[:, None]
    return (unit_vec, inverse, unit_vec.astype(jnp.bfloat16))


def norm_back(upstream, unit_vec, inverse):
    inner_prod = jnp.sum(unit_vec * upstream, axis=1, keepdims=True)
    return (inverse[:, None] * (upstream - unit_vec * inner_prod)).astype(jnp.bfloat16)


def shift_all(x, axis):
    size = lax.axis_size(axis)
    index = lax.axis_index(axis)
    got = [x]
    for s in range(1, size):
        got.append(lax.ppermute(x, axis, [(i, (i + s) % size) for i in range(size)]))
    order = (index - jnp.arange(size)) % size
    return jax.tree.map(lambda *xs: jnp.take(jnp.stack(xs, axis=0), order, axis=0), *got)


def exchange(parts, axis):
    size = lax.axis_size(axis)
    index = lax.axis_index(axis)
    got = [jnp.take(parts, index, axis=0)]
    for s in range(1, size):
        sent = jnp.take(parts, (index + s) % size, axis=0)
        got.append(lax.ppermute(sent, axis, [(i, (i + s) % size) for i in range(size)]))
    stacked = jnp.stack(got, axis=0)
    return jnp.take(stacked, (index - jnp.arange(size)) % size, axis=0)


def body(query_feat, code_feat, projection, hard_ids, loss_weight):
    groups = lax.axis_size("group")
    members = lax.axis_size("member")
    group_index = lax.axis_index("group")
    member_index = lax.axis_index("member")
    queries_dev = query_feat.shape[0]
    feat_width = query_feat.shape[1]
    emb_width = projection.shape[1]
    slot_count = queries_dev // CB
    per_group = members * slot_count
    group_span = members * queries_dev
    rows_dev = feat_width // (groups * members)

    feats = jnp.stack([query_feat, code_feat], axis=0).reshape(
        2, queries_dev, groups, members, rows_dev
    )
    feats = jnp.transpose(feats, (3, 0, 1, 2, 4))
    feat_cols = lax.all_to_all(feats, "member", split_axis=0, concat_axis=0, tiled=True)

    q_unit, q_inv, q_emb = embed(query_feat, projection)
    code_values = lax.all_gather(
        jnp.dot(code_feat, projection, preferred_element_type=jnp.float32),
        "member",
        axis=0,
        tiled=True,
    )
    c_inv = lax.rsqrt(jnp.sum(code_values * code_values, axis=1) + epsilon)
    c_unit = code_values * c_inv[:, None]
    group_codes = c_unit.astype(jnp.bfloat16)
    q_all = lax.all_to_all(
        jnp.broadcast_to(q_emb[None], (groups, queries_dev, emb_width)),
        "group",
        split_axis=0,
        concat_axis=0,
        tiled=True,
    )
    ids_all = shift_all(hard_ids[0], "group")

    block_ids = group_index * per_group + jnp.arange(per_group, dtype=jnp.int32)
    asked = jnp.any(ids_all[:, :, None] == block_ids[None, None, :], axis=1)
    own = jnp.arange(groups, dtype=jnp.int32) == group_index
    block_mask = asked | own[:, None]
    col_mask = jnp.broadcast_to(
        block_mask[:, :, None], (groups, per_group, CB)
    ).reshape(groups, 1, group_span)

    scores = inverse_temp * jnp.einsum(
        "gqe,ke->gqk", q_all, group_codes, preferred_element_type=jnp.float32
    )
    scores = jnp.where(col_mask, scores, -jnp.inf)
    part_max = jnp.max(scores, axis=2)
    safe_max = jnp.where(part_max > -jnp.inf, part_max, 0.0)
    part_sum = jnp.sum(jnp.exp(scores - safe_max[:, :, None]), axis=2)
    weights_row = jnp.broadcast_to(loss_weight[None], (groups, queries_dev))
    stats = shift_all(jnp.stack([part_max, part_sum, weights_row], axis=0), "group")
    w_all = stats[:, 2, 0]
    row_max = jnp.max(stats[:, 0], axis=0)
    row_sum = jnp.sum(stats[:, 1] * jnp.exp(stats[:, 0] - row_max[None]), axis=0)
    log_total = row_max + jnp.log(row_sum)

    offsets = jnp.arange(queries_dev, dtype=jnp.int32)
    columns = jnp.arange(group_span, dtype=jnp.int32)
    positive = (columns[None, :] == (member_index * queries_dev + offsets)[:, None]).astype(
        jnp.float32
    )
    positive = positive[None] * own[:, None, None].astype(jnp.float32)
    factor = w_all * inverse_temp
    grad = (
        factor[:, :, None] * (jnp.exp(scores - log_total[:, :, None]) - positive)
    ).astype(jnp.bfloat16)

    code_terms = None
    for g in range(groups):
        term = jnp.dot(grad[g].T, q_all[g], preferred_element_type=jnp.float32)
        term = jnp.where(g == group_index, term, term.astype(jnp.bfloat16).astype(jnp.float32))
        code_terms = term if code_terms is None else code_terms + term
    code_sum = code_terms.astype(jnp.bfloat16)
    grad_dq, code_sum = lax.optimization_barrier((grad, code_sum))
    code_delta = lax.psum(code_sum, "member").astype(jnp.float32)
    delta_parts = jnp.einsum("gqk,ke->gqe", grad_dq, group_codes, preferred_element_type=jnp.float32)
    returned = exchange(delta_parts.astype(jnp.bfloat16), "group").astype(jnp.float32)
    own_part = jnp.take(delta_parts, group_index, axis=0)
    query_delta = own_part + jnp.sum(jnp.where(own[:, None, None], 0.0, returned), axis=0)


    dz_query = norm_back(query_delta, q_unit, q_inv)
    dz_code_all = norm_back(code_delta, c_unit, c_inv)
    dz_code = lax.dynamic_slice_in_dim(dz_code_all, member_index * queries_dev, queries_dev, 0)
    query_grad = jnp.einsum(
        "qe,de->qd", dz_query, projection, preferred_element_type=jnp.float32
    ).astype(jnp.bfloat16)
    code_grad = jnp.einsum(
        "qe,de->qd", dz_code, projection, preferred_element_type=jnp.float32
    ).astype(jnp.bfloat16)

    dzq_all = lax.all_to_all(
        jnp.broadcast_to(dz_query[None], (members, queries_dev, emb_width)),
        "member",
        split_axis=0,
        concat_axis=0,
        tiled=True,
    )
    dzc_all = dz_code_all.reshape(members, queries_dev, emb_width)
    proj_parts = jnp.einsum(
        "mqgr,mqe->gre", feat_cols[:, 0], dzq_all, preferred_element_type=jnp.float32
    ) + jnp.einsum("mqgr,mqe->gre", feat_cols[:, 1], dzc_all, preferred_element_type=jnp.float32)
    own_proj = jnp.take(proj_parts, group_index, axis=0)
    sent_proj = jnp.where(own[:, None, None], 0.0, proj_parts).astype(jnp.bfloat16)
    projection_grad = own_proj + lax.psum_scatter(
        sent_proj, "group", scatter_dimension=0, tiled=True
    ).reshape(rows_dev, emb_width).astype(jnp.float32)
    return (query_grad, code_grad, projection_grad)


def solution(mesh):
    return jax.shard_map(
        body,
        mesh=mesh,
        in_specs=(
            P(("group", "member"), None),
            P(("group", "member"), None),
            P(),
            P(("group", "member"), None),
            P(("group", "member")),
        ),
        out_specs=(
            P(("group", "member"), None),
            P(("group", "member"), None),
            P(("group", "member"), None),
        ),
        check_vma=False,
    )
```

```python
import jax
import jax.numpy as jnp
from jax import lax
from jax.sharding import PartitionSpec as P

CB = 64


inverse_temp = 120.0
epsilon = 1e-06


def embed(features, projection):
    values = jnp.dot(features, projection, preferred_element_type=jnp.float32)
    inverse = lax.rsqrt(jnp.sum(values * values, axis=1) + epsilon)
    unit_vec = values * inverse[:, None]
    return (unit_vec, inverse, unit_vec.astype(jnp.bfloat16))


def norm_back(upstream, unit_vec, inverse):
    inner_prod = jnp.sum(unit_vec * upstream, axis=1, keepdims=True)
    return (inverse[:, None] * (upstream - unit_vec * inner_prod)).astype(jnp.bfloat16)


def shift_all(x, axis):
    size = lax.axis_size(axis)
    index = lax.axis_index(axis)
    got = [x]
    for s in range(1, size):
        got.append(lax.ppermute(x, axis, [(i, (i + s) % size) for i in range(size)]))
    order = (index - jnp.arange(size)) % size
    return jax.tree.map(lambda *xs: jnp.take(jnp.stack(xs, axis=0), order, axis=0), *got)


def exchange(parts, axis):
    size = lax.axis_size(axis)
    index = lax.axis_index(axis)
    got = [jnp.take(parts, index, axis=0)]
    for s in range(1, size):
        sent = jnp.take(parts, (index + s) % size, axis=0)
        got.append(lax.ppermute(sent, axis, [(i, (i + s) % size) for i in range(size)]))
    stacked = jnp.stack(got, axis=0)
    return jnp.take(stacked, (index - jnp.arange(size)) % size, axis=0)


def body(query_feat, code_feat, projection, hard_ids, loss_weight):
    groups = lax.axis_size("group")
    members = lax.axis_size("member")
    group_index = lax.axis_index("group")
    member_index = lax.axis_index("member")
    queries_dev = query_feat.shape[0]
    feat_width = query_feat.shape[1]
    emb_width = projection.shape[1]
    slot_count = queries_dev // CB
    per_group = members * slot_count
    group_span = members * queries_dev
    rows_dev = feat_width // (groups * members)

    feats = jnp.stack([query_feat, code_feat], axis=0).reshape(
        2, queries_dev, groups, members, rows_dev
    )
    feats = jnp.transpose(feats, (3, 0, 1, 2, 4))
    feat_cols = lax.all_to_all(feats, "member", split_axis=0, concat_axis=0, tiled=True)

    q_unit, q_inv, q_emb = embed(query_feat, projection)
    code_values = lax.all_gather(
        jnp.dot(code_feat, projection, preferred_element_type=jnp.float32),
        "member",
        axis=0,
        tiled=True,
    )
    c_inv = lax.rsqrt(jnp.sum(code_values * code_values, axis=1) + epsilon)
    c_unit = code_values * c_inv[:, None]
    group_codes = c_unit.astype(jnp.bfloat16)
    q_all = lax.all_to_all(
        jnp.broadcast_to(q_emb[None], (groups, queries_dev, emb_width)),
        "group",
        split_axis=0,
        concat_axis=0,
        tiled=True,
    )
    ids_all = shift_all(hard_ids[0], "group")

    block_ids = group_index * per_group + jnp.arange(per_group, dtype=jnp.int32)
    asked = jnp.any(ids_all[:, :, None] == block_ids[None, None, :], axis=1)
    own = jnp.arange(groups, dtype=jnp.int32) == group_index
    block_mask = asked | own[:, None]
    col_mask = jnp.broadcast_to(
        block_mask[:, :, None], (groups, per_group, CB)
    ).reshape(groups, 1, group_span)

    scores = inverse_temp * jnp.einsum(
        "gqe,ke->gqk", q_all, group_codes, preferred_element_type=jnp.float32
    )
    scores = jnp.where(col_mask, scores, -jnp.inf)
    part_max = jnp.max(scores, axis=2)
    safe_max = jnp.where(part_max > -jnp.inf, part_max, 0.0)
    part_sum = jnp.sum(jnp.exp(scores - safe_max[:, :, None]), axis=2)
    weights_row = jnp.broadcast_to(loss_weight[None], (groups, queries_dev))
    stats = shift_all(jnp.stack([part_max, part_sum, weights_row], axis=0), "group")
    w_all = stats[:, 2, 0]
    row_max = jnp.max(stats[:, 0], axis=0)
    row_sum = jnp.sum(stats[:, 1] * jnp.exp(stats[:, 0] - row_max[None]), axis=0)
    log_total = row_max + jnp.log(row_sum)

    offsets = jnp.arange(queries_dev, dtype=jnp.int32)
    columns = jnp.arange(group_span, dtype=jnp.int32)
    positive = (columns[None, :] == (member_index * queries_dev + offsets)[:, None]).astype(
        jnp.float32
    )
    positive = positive[None] * own[:, None, None].astype(jnp.float32)
    factor = w_all * inverse_temp
    grad = (
        factor[:, :, None] * (jnp.exp(scores - log_total[:, :, None]) - positive)
    ).astype(jnp.bfloat16)

    code_terms = None
    for g in range(groups):
        term = jnp.dot(grad[g].T, q_all[g], preferred_element_type=jnp.float32)
        term = jnp.where(g == group_index, term, term.astype(jnp.bfloat16).astype(jnp.float32))
        code_terms = term if code_terms is None else code_terms + term
    code_sum = code_terms.astype(jnp.bfloat16)
    grad_dq, code_sum = lax.optimization_barrier((grad, code_sum))
    code_delta = lax.psum(code_sum, "member").astype(jnp.float32)
    delta_parts = jnp.einsum("gqk,ke->gqe", grad_dq, group_codes, preferred_element_type=jnp.float32)
    returned = exchange(delta_parts.astype(jnp.bfloat16), "group").astype(jnp.float32)
    own_part = jnp.take(delta_parts, group_index, axis=0)
    query_delta = own_part + jnp.sum(jnp.where(own[:, None, None], 0.0, returned), axis=0)


    dz_query = norm_back(query_delta, q_unit, q_inv)
    dz_code_all = norm_back(code_delta, c_unit, c_inv)
    dz_code = lax.dynamic_slice_in_dim(dz_code_all, member_index * queries_dev, queries_dev, 0)
    query_grad = jnp.einsum(
        "qe,de->qd", dz_query, projection, preferred_element_type=jnp.float32
    ).astype(jnp.bfloat16)
    code_grad = jnp.einsum(
        "qe,de->qd", dz_code, projection, preferred_element_type=jnp.float32
    ).astype(jnp.bfloat16)

    dzq_all = lax.all_to_all(
        jnp.broadcast_to(dz_query[None], (members, queries_dev, emb_width)),
        "member",
        split_axis=0,
        concat_axis=0,
        tiled=True,
    )
    dzc_all = dz_code_all.reshape(members, queries_dev, emb_width)
    proj_parts = jnp.einsum(
        "mqgr,mqe->gre", feat_cols[:, 0], dzq_all, preferred_element_type=jnp.float32
    ) + jnp.einsum("mqgr,mqe->gre", feat_cols[:, 1], dzc_all, preferred_element_type=jnp.float32)
    projection_grad = lax.psum_scatter(
        proj_parts.astype(jnp.bfloat16), "group", scatter_dimension=0, tiled=True
    ).reshape(rows_dev, emb_width).astype(jnp.float32)
    return (query_grad, code_grad, projection_grad)


def solution(mesh):
    return jax.shard_map(
        body,
        mesh=mesh,
        in_specs=(
            P(("group", "member"), None),
            P(("group", "member"), None),
            P(),
            P(("group", "member"), None),
            P(("group", "member")),
        ),
        out_specs=(
            P(("group", "member"), None),
            P(("group", "member"), None),
            P(("group", "member"), None),
        ),
        check_vma=False,
    )
```
